32 devices in a mesh: dp: 4 (over y, core), seq: 8 (over z, x).
Axes of the slice: x: 2, y: 2, z: 4, core: 2. Of those that a mesh axis runs over, the one named last changes fastest.
Arguments:
- layer_input: bfloat16 [4, 4096, 1024], P('dp', 'seq'), may hold values from -28 to 28
- w_query: bfloat16 [1024, 1024], replicated, may hold values from -0.1875 to 0.1875
- w_key: bfloat16 [1024, 1024], replicated, may hold values from -0.1875 to 0.1875
- w_value: bfloat16 [1024, 1024], replicated, may hold values from -0.1875 to 0.1875
- w_out: bfloat16 [1024, 1024], replicated, may hold values from -0.1875 to 0.1875
- offsets: int32 [3], replicated, may hold values from 0 to 3
- grad_out: bfloat16 [4, 4096, 1024], P('dp', 'seq'), may hold values from -6 to 6
Outputs:
- layer_output: bfloat16 [4, 4096, 1024], P('dp', 'seq')
- grad_x: bfloat16 [4, 4096, 1024], P('dp', 'seq')
- grad_query: float32 [1024, 1024], P('seq')
- grad_key: float32 [1024, 1024], P('seq')
- grad_value: float32 [1024, 1024], P('seq')
- grad_outw: float32 [1024, 1024], P('seq')
The draws below stay inside these ranges and needn't reach their ends.
All inputs are finite; a program needn't handle non-finite values.
Results may differ from the reference program's by a relative error of at most 0.018.
The reference program's roundings to bfloat16 on the way count: a program that leaves them out, or rounds other values in their place, can miss the bound.
Values may be sent and summed in bfloat16 or wider, within the bound.
No kernel may reach another device: no remote copies, remote signals or barrier semaphores. Data moves between devices by JAX's collectives and lax.ppermute only.
A program may use at most 192 MiB of HBM per device.

```python
import jax
import jax.numpy as jnp
from jax import lax

D = 1024
HEADS = 16
BLOCK = 128
TOK_DEV = 512
HEAD = 64
LEVELS = 3
BLK_DEV = 4
DOCS = 4
LEN = 4096
N_SEQ = 8


def draw_layer_input(key, part):
    first = jax.random.fold_in(key, 0)
    values = jnp.clip(jax.random.normal(first, (DOCS, LEN, D), jnp.float32), -6.0, 6.0)
    return values.astype(jnp.bfloat16)


def block_scale(own_key, dims, cuts, least, largest):
    def one(axis_at, blocks):
        draws = jax.random.uniform(jax.random.fold_in(jax.random.fold_in(own_key, 6), axis_at), (blocks,), jnp.float32, least / len(cuts), largest / len(cuts))
        return jnp.repeat(jnp.exp(draws), dims[axis_at] // blocks).reshape((-1,) + (1,) * (len(dims) - axis_at - 1))

    gain = one(*cuts[0])
    for cut in cuts[1:]:
        gain = gain * one(*cut)
    return gain


def bell_draw(key, shape, spread, limit, cuts=(), kind=jnp.bfloat16):
    values = jax.random.normal(key, shape, jnp.float32) * spread
    if len(cuts) > 0:
        values = block_scale(key, shape, cuts, -0.22, 0.18) * values
    return jnp.clip(values, min=-limit, max=limit).astype(kind)


def setup_inputs(seed: int = 0) -> dict:
    key_of = jax.random.split(jax.random.key(seed), 8)
    return {
        "layer_input": draw_layer_input(jax.random.fold_in(key_of[7], 71), 0),
        "w_query": bell_draw(key_of[1], (D, D), D ** -0.5, 0.1875),
        "w_key": bell_draw(key_of[2], (D, D), D ** -0.5, 0.1875),
        "w_value": bell_draw(key_of[3], (D, D), D ** -0.5, 0.1875),
        "w_out": bell_draw(key_of[4], (D, D), D ** -0.5, 0.1875),
        "offsets": jax.random.randint(key_of[5], (LEVELS,), 0, BLK_DEV).astype(jnp.int32),
        "grad_out": bell_draw(key_of[6], (DOCS, LEN, D), 1.0, 6.0, ((0, 4), (1, 8))),
    }


def heads_of(a):
    return a.astype(jnp.float32).reshape(a.shape[0], HEADS, HEAD)


def shard_attention(query, keys, values, d_att):
    scale = HEAD ** -0.5
    scores = jnp.einsum("qhe,khe->hqk", heads_of(query), heads_of(keys)) * scale
    top = jnp.max(scores, axis=-1, keepdims=True)
    lse = top + jnp.log(jnp.sum(jnp.exp(scores - top), axis=-1, keepdims=True))
    prob = jnp.exp(scores - lse)
    prob_b = prob.astype(jnp.bfloat16)
    att = jnp.einsum("hqk,khe->qhe", prob_b.astype(jnp.float32), heads_of(values))
    att = att.reshape(query.shape[0], D).astype(jnp.bfloat16)
    dprob = jnp.einsum("qhe,khe->hqk", heads_of(d_att), heads_of(values))
    delta = jnp.sum(prob * dprob, axis=-1, keepdims=True)
    dsc = (prob * (dprob - delta) * scale).astype(jnp.bfloat16).astype(jnp.float32)
    dq = jnp.einsum("hqk,khe->qhe", dsc, heads_of(keys)).reshape(query.shape[0], D).astype(jnp.bfloat16)
    dk = jnp.einsum("hqk,qhe->khe", dsc, heads_of(query)).reshape(keys.shape[0], D)
    dv = jnp.einsum("hqk,qhe->khe", prob_b.astype(jnp.float32), heads_of(d_att)).reshape(keys.shape[0], D)
    return att, dq, dk, dv


def reference(layer_input, w_query, w_key, w_value, w_out, offsets, grad_out):
    outs_y = []
    outs_dx = []
    grads = [jnp.zeros((D, D), jnp.float32) for index in range(4)]
    for doc in range(DOCS):
        rows = layer_input[doc]
        cot = grad_out[doc]
        query = jnp.dot(rows, w_query, preferred_element_type=jnp.float32).astype(jnp.bfloat16)
        keys = jnp.dot(rows, w_key, preferred_element_type=jnp.float32).astype(jnp.bfloat16)
        values = jnp.dot(rows, w_value, preferred_element_type=jnp.float32).astype(jnp.bfloat16)
        d_att = jnp.dot(cot, w_out.T, preferred_element_type=jnp.float32).astype(jnp.bfloat16)

        def one_shard(shard):
            first = (shard * TOK_DEV).astype(jnp.int32)
            key_list = [lax.dynamic_slice_in_dim(keys, first, TOK_DEV, 0)]
            value_list = [lax.dynamic_slice_in_dim(values, first, TOK_DEV, 0)]
            for level in range(LEVELS):
                partner = jnp.bitwise_xor(shard, jnp.int32(1 << level))
                start = (partner * TOK_DEV + offsets[level] * BLOCK).astype(jnp.int32)
                key_list.append(lax.dynamic_slice_in_dim(keys, start, BLOCK, 0))
                value_list.append(lax.dynamic_slice_in_dim(values, start, BLOCK, 0))
            return shard_attention(lax.dynamic_slice_in_dim(query, first, TOK_DEV, 0),
                                   jnp.concatenate(key_list, 0), jnp.concatenate(value_list, 0),
                                   lax.dynamic_slice_in_dim(d_att, first, TOK_DEV, 0))

        att, dq, dk_all, dv_all = lax.map(one_shard, jnp.arange(N_SEQ, dtype=jnp.int32))
        dk_sh = dk_all[:, :TOK_DEV]
        dv_sh = dv_all[:, :TOK_DEV]
        shards = jnp.arange(N_SEQ, dtype=jnp.int32)
        for level in range(LEVELS):
            source = jnp.bitwise_xor(shards, jnp.int32(1 << level))
            lo = TOK_DEV + level * BLOCK
            rem_k = dk_all[:, lo:lo + BLOCK][source]
            rem_v = dv_all[:, lo:lo + BLOCK][source]
            start = (offsets[level] * BLOCK).astype(jnp.int32)
            dk_sh = lax.dynamic_update_slice_in_dim(dk_sh, lax.dynamic_slice_in_dim(dk_sh, start, BLOCK, 1) + rem_k, start, 1)
            dv_sh = lax.dynamic_update_slice_in_dim(dv_sh, lax.dynamic_slice_in_dim(dv_sh, start, BLOCK, 1) + rem_v, start, 1)
        att = att.reshape(LEN, D)
        dq = dq.reshape(LEN, D)
        dk = dk_sh.reshape(LEN, D).astype(jnp.bfloat16)
        dv = dv_sh.reshape(LEN, D).astype(jnp.bfloat16)
        outs_y.append(jnp.dot(att, w_out, preferred_element_type=jnp.float32).astype(jnp.bfloat16))
        total = jnp.dot(dq, w_query.T, preferred_element_type=jnp.float32)
        total = total + jnp.dot(dk, w_key.T, preferred_element_type=jnp.float32)
        total = total + jnp.dot(dv, w_value.T, preferred_element_type=jnp.float32)
        outs_dx.append(total.astype(jnp.bfloat16))
        grads[0] = grads[0] + jnp.dot(rows.T, dq, preferred_element_type=jnp.float32)
        grads[1] = grads[1] + jnp.dot(rows.T, dk, preferred_element_type=jnp.float32)
        grads[2] = grads[2] + jnp.dot(rows.T, dv, preferred_element_type=jnp.float32)
        grads[3] = grads[3] + jnp.dot(att.T, cot, preferred_element_type=jnp.float32)
    return (jnp.stack(outs_y), jnp.stack(outs_dx), grads[0], grads[1], grads[2], grads[3])
```

```python
import functools

import jax
import jax.numpy as jnp
from jax import lax
from jax.experimental import pallas as pl
from jax.experimental.pallas import tpu as pltpu
from jax.sharding import PartitionSpec as P

HEADS = 16
BLOCK = 128
LANES = 128


def partner(array, axis, apart):
    return lax.ppermute(array, axis, [(i, i ^ 1 << apart) for i in range(lax.axis_size(axis))])


def swap_blocks(keys_local, values_local, offsets, levels):
    remote = []
    for level in range(levels):
        start = offsets[level] * BLOCK
        pair = jnp.stack(
            [
                lax.dynamic_slice_in_dim(keys_local, start, BLOCK, 0),
                lax.dynamic_slice_in_dim(values_local, start, BLOCK, 0),
            ]
        )
        remote.append(partner(pair, "seq", level))
    return remote


def attention_kernel(q_ref, k_ref, v_ref, do_ref, att_ref, dq_ref, dk_ref, dv_ref, *, head, scale):
    q = q_ref[...]
    k = k_ref[...]
    v = v_ref[...]
    do = do_ref[...]
    width = q.shape[1]
    lane = lax.broadcasted_iota(jnp.int32, (1, width), 1)
    outs = None
    for j in range(width // head):
        inside = (lane >= j * head) & (lane < (j + 1) * head)
        qm = jnp.where(inside, q * jnp.asarray(scale, q.dtype), jnp.zeros_like(q))
        dom = jnp.where(inside, do, jnp.zeros_like(do))
        s = lax.dot_general(qm, k, (((1,), (1,)), ((), ())), preferred_element_type=jnp.float32)
        top = jnp.max(s, axis=-1, keepdims=True)
        e = jnp.exp(s - top)
        p = e * (1.0 / jnp.sum(e, axis=-1, keepdims=True))
        pb = p.astype(jnp.bfloat16)
        a = jnp.dot(pb, v, preferred_element_type=jnp.float32)
        dp = lax.dot_general(dom, v, (((1,), (1,)), ((), ())), preferred_element_type=jnp.float32)
        delta = jnp.sum(p * dp, axis=-1, keepdims=True)
        ds = (p * (dp - delta) * scale).astype(jnp.bfloat16)
        dq = jnp.dot(ds, k, preferred_element_type=jnp.float32)
        dk = lax.dot_general(ds, q, (((0,), (0,)), ((), ())), preferred_element_type=jnp.float32)
        dv = lax.dot_general(pb, do, (((0,), (0,)), ((), ())), preferred_element_type=jnp.float32)
        if outs is None:
            outs = [a, dq, dk, dv]
        else:
            outs = [jnp.where(inside, new, old) for new, old in zip([a, dq, dk, dv], outs)]
    att_ref[...] = outs[0].astype(att_ref.dtype)
    dq_ref[...] = outs[1].astype(dq_ref.dtype)
    dk_ref[...] = outs[2]
    dv_ref[...] = outs[3]


def attention(query, keys, values, d_att, head):
    tok, width = query.shape
    total = keys.shape[0]
    steps = width // LANES
    qspec = pl.BlockSpec((tok, LANES), lambda i: (0, i))
    kspec = pl.BlockSpec((total, LANES), lambda i: (0, i))
    return pl.pallas_call(
        functools.partial(attention_kernel, head=head, scale=head ** -0.5),
        grid=(steps,),
        in_specs=[qspec, kspec, kspec, qspec],
        out_specs=[qspec, qspec, kspec, kspec],
        out_shape=[
            jax.ShapeDtypeStruct((tok, width), jnp.bfloat16),
            jax.ShapeDtypeStruct((tok, width), jnp.bfloat16),
            jax.ShapeDtypeStruct((total, width), jnp.float32),
            jax.ShapeDtypeStruct((total, width), jnp.float32),
        ],
        compiler_params=pltpu.CompilerParams(vmem_limit_bytes=60 * 1024 * 1024),
        cost_estimate=pl.CostEstimate(
            flops=12 * tok * total * width * (LANES // head),
            transcendentals=tok * total * (width // head),
            bytes_accessed=4 * tok * width + 12 * total * width,
        ),
    )(query, keys, values, d_att)


def gradient_terms(sources):
    parts = []
    for left, right in sources:
        parts.append(jnp.dot(left.T, right, preferred_element_type=jnp.float32))
    return jnp.concatenate(parts, axis=1)


def reduce_gradients(terms):
    n_dp = lax.axis_size("dp")
    half = terms.shape[1] // 2
    core = lax.axis_index("dp") % 2
    mine = lax.dynamic_slice_in_dim(terms, core * half, half, 1)
    other = lax.dynamic_slice_in_dim(terms, (1 - core) * half, half, 1)
    got = lax.ppermute(other.astype(jnp.bfloat16), "dp", [(i, i ^ 1) for i in range(n_dp)])
    summed = (mine + got.astype(jnp.float32)).astype(jnp.bfloat16)
    part = lax.psum_scatter(summed, "seq", scatter_dimension=0, tiled=True)
    if n_dp > 2:
        across = lax.ppermute(part, "dp", [(i, i ^ 2) for i in range(n_dp)])
        part = (part.astype(jnp.float32) + across.astype(jnp.float32)).astype(jnp.bfloat16)
    back = lax.ppermute(part, "dp", [(i, i ^ 1) for i in range(n_dp)])
    first = jnp.where(core == 0, part, back)
    second = jnp.where(core == 0, back, part)
    return jnp.concatenate([first, second], axis=1).astype(jnp.float32)


def body(layer_input, w_query, w_key, w_value, w_out, offsets, grad_out):
    rows = layer_input[0]
    cot = grad_out[0]
    tok = rows.shape[0]
    width = rows.shape[1]
    head = width // HEADS
    levels = lax.axis_size("seq").bit_length() - 1
    query = jnp.dot(rows, w_query, preferred_element_type=jnp.float32).astype(jnp.bfloat16)
    keys_local = jnp.dot(rows, w_key, preferred_element_type=jnp.float32).astype(jnp.bfloat16)
    values_local = jnp.dot(rows, w_value, preferred_element_type=jnp.float32).astype(jnp.bfloat16)
    remote = swap_blocks(keys_local, values_local, offsets, levels)
    all_keys = jnp.concatenate([keys_local] + [piece[0] for piece in remote], 0)
    all_values = jnp.concatenate([values_local] + [piece[1] for piece in remote], 0)
    d_att = jnp.dot(cot, w_out.T, preferred_element_type=jnp.float32).astype(jnp.bfloat16)
    attended, dquery, dk_acc, dv_acc = attention(query, all_keys, all_values, d_att, head)
    result = jnp.dot(attended, w_out, preferred_element_type=jnp.float32).astype(jnp.bfloat16)
    dkey_sum = dk_acc[:tok]
    dvalue_sum = dv_acc[:tok]
    for level in range(levels):
        low = tok + level * BLOCK
        piece = jnp.stack([dk_acc[low : low + BLOCK], dv_acc[low : low + BLOCK]])
        returned = partner(piece.astype(jnp.bfloat16), "seq", level).astype(piece.dtype)
        start = offsets[level] * BLOCK
        dkey_sum = lax.dynamic_update_slice_in_dim(
            dkey_sum, lax.dynamic_slice_in_dim(dkey_sum, start, BLOCK, 0) + returned[0], start, 0
        )
        dvalue_sum = lax.dynamic_update_slice_in_dim(
            dvalue_sum,
            lax.dynamic_slice_in_dim(dvalue_sum, start, BLOCK, 0) + returned[1],
            start,
            0,
        )
    dkey = dkey_sum.astype(jnp.bfloat16)
    dvalue = dvalue_sum.astype(jnp.bfloat16)
    total = jnp.dot(dquery, w_query.T, preferred_element_type=jnp.float32)
    total = total + jnp.dot(dkey, w_key.T, preferred_element_type=jnp.float32)
    total = total + jnp.dot(dvalue, w_value.T, preferred_element_type=jnp.float32)
    grad_input = total.astype(jnp.bfloat16)
    sources = ((rows, dquery), (rows, dkey), (rows, dvalue), (attended, cot))
    summed = reduce_gradients(gradient_terms(sources))
    return (
        result[None],
        grad_input[None],
        summed[:, :width],
        summed[:, width : 2 * width],
        summed[:, 2 * width : 3 * width],
        summed[:, 3 * width :],
    )


def solution(mesh):
    return jax.shard_map(
        body,
        mesh=mesh,
        in_specs=(P("dp", "seq", None), P(), P(), P(), P(), P(), P("dp", "seq", None)),
        out_specs=(
            P("dp", "seq", None),
            P("dp", "seq", None),
            P("seq", None),
            P("seq", None),
            P("seq", None),
            P("seq", None),
        ),
        check_vma=False,
    )
```

```python
import functools

import jax
import jax.numpy as jnp
from jax import lax
from jax.experimental import pallas as pl
from jax.experimental.pallas import tpu as pltpu
from jax.sharding import PartitionSpec as P

HEADS = 16
BLOCK = 128
LANES = 128


def partner(array, axis, apart):
    return lax.ppermute(array, axis, [(i, i ^ 1 << apart) for i in range(lax.axis_size(axis))])


def swap_blocks(keys_local, values_local, offsets, levels):
    remote = []
    for level in range(levels):
        start = offsets[level] * BLOCK
        pair = jnp.stack(
            [
                lax.dynamic_slice_in_dim(keys_local, start, BLOCK, 0),
                lax.dynamic_slice_in_dim(values_local, start, BLOCK, 0),
            ]
        )
        remote.append(partner(pair, "seq", level))
    return remote


def attention_kernel(q_ref, k_ref, v_ref, do_ref, att_ref, dq_ref, dk_ref, dv_ref, *, head, scale):
    q = q_ref[...]
    k = k_ref[...]
    v = v_ref[...]
    do = do_ref[...]
    width = q.shape[1]
    lane = lax.broadcasted_iota(jnp.int32, (1, width), 1)
    outs = None
    for j in range(width // head):
        inside = (lane >= j * head) & (lane < (j + 1) * head)
        qm = jnp.where(inside, q * jnp.asarray(scale, q.dtype), jnp.zeros_like(q))
        dom = jnp.where(inside, do, jnp.zeros_like(do))
        s = lax.dot_general(qm, k, (((1,), (1,)), ((), ())), preferred_element_type=jnp.float32)
        top = jnp.max(s, axis=-1, keepdims=True)
        e = jnp.exp(s - top)
        p = e * (1.0 / jnp.sum(e, axis=-1, keepdims=True))
        pb = p.astype(jnp.bfloat16)
        a = jnp.dot(pb, v, preferred_element_type=jnp.float32)
        dp = lax.dot_general(dom, v, (((1,), (1,)), ((), ())), preferred_element_type=jnp.float32)
        delta = jnp.sum(p * dp, axis=-1, keepdims=True)
        ds = (p * (dp - delta) * scale).astype(jnp.bfloat16)
        dq = jnp.dot(ds, k, preferred_element_type=jnp.float32)
        dk = lax.dot_general(ds, q, (((0,), (0,)), ((), ())), preferred_element_type=jnp.float32)
        dv = lax.dot_general(pb, do, (((0,), (0,)), ((), ())), preferred_element_type=jnp.float32)
        if outs is None:
            outs = [a, dq, dk, dv]
        else:
            outs = [jnp.where(inside, new, old) for new, old in zip([a, dq, dk, dv], outs)]
    att_ref[...] = outs[0].astype(att_ref.dtype)
    dq_ref[...] = outs[1].astype(dq_ref.dtype)
    dk_ref[...] = outs[2]
    dv_ref[...] = outs[3]


def attention(query, keys, values, d_att, head):
    tok, width = query.shape
    total = keys.shape[0]
    steps = width // LANES
    qspec = pl.BlockSpec((tok, LANES), lambda i: (0, i))
    kspec = pl.BlockSpec((total, LANES), lambda i: (0, i))
    return pl.pallas_call(
        functools.partial(attention_kernel, head=head, scale=head ** -0.5),
        grid=(steps,),
        in_specs=[qspec, kspec, kspec, qspec],
        out_specs=[qspec, qspec, kspec, kspec],
        out_shape=[
            jax.ShapeDtypeStruct((tok, width), jnp.bfloat16),
            jax.ShapeDtypeStruct((tok, width), jnp.bfloat16),
            jax.ShapeDtypeStruct((total, width), jnp.float32),
            jax.ShapeDtypeStruct((total, width), jnp.float32),
        ],
        compiler_params=pltpu.CompilerParams(vmem_limit_bytes=60 * 1024 * 1024),
        cost_estimate=pl.CostEstimate(
            flops=12 * tok * total * width * (LANES // head),
            transcendentals=tok * total * (width // head),
            bytes_accessed=4 * tok * width + 12 * total * width,
        ),
    )(query, keys, values, d_att)


def gradient_terms(sources):
    parts = []
    for left, right in sources:
        parts.append(jnp.dot(left.T, right, preferred_element_type=jnp.float32).astype(jnp.bfloat16))
    return jnp.concatenate(parts, axis=1)


def exchange(array, axis, mask):
    return lax.ppermute(array, axis, [(i, i ^ mask) for i in range(lax.axis_size(axis))])


def add_bf16(a, b):
    return (a.astype(jnp.float32) + b.astype(jnp.float32)).astype(jnp.bfloat16)


def halve(data, steps):
    for kind, axis, mask, bit, at in steps:
        keep = lax.dynamic_index_in_dim(data, bit, at, keepdims=False)
        send = lax.dynamic_index_in_dim(data, 1 - bit, at, keepdims=False)
        data = add_bf16(keep, exchange(send, axis, mask))
    return data


def reduce_gradients(terms):
    n_dp = lax.axis_size("dp")
    n_seq = lax.axis_size("seq")
    seq_bits = n_seq.bit_length() - 1
    dp_bits = n_dp.bit_length() - 1
    rows, width = terms.shape
    half = width // 2
    blk = rows // n_seq
    dp_i = lax.axis_index("dp")
    seq_i = lax.axis_index("seq")
    core = dp_i % 2
    mine = lax.dynamic_slice_in_dim(terms, core * half, half, 1)
    other = lax.dynamic_slice_in_dim(terms, (1 - core) * half, half, 1)
    summed = add_bf16(mine, exchange(other, "dp", 1))
    dims = [("seq", 0)] + [("dp", b) for b in range(1, dp_bits)] + [("seq", b) for b in range(1, seq_bits)]
    first = dims[:3]
    n_parts = len(first)
    cuts = [(half // LANES) * p // n_parts * LANES for p in range(n_parts + 1)]
    pieces = []
    for p in range(n_parts):
        order = first[p:] + first[:p] + dims[3:]
        data = summed[:, cuts[p] : cuts[p + 1]]
        data = data.reshape([2] * seq_bits + [2] * (dp_bits - 1) + [blk >> (dp_bits - 1), cuts[p + 1] - cuts[p]])
        steps = []
        removed = []
        for axis, b in order:
            if axis == "seq":
                at = seq_bits - 1 - b
                bit = (seq_i >> b) % 2
            else:
                at = seq_bits + (dp_bits - 1 - b)
                bit = (dp_i >> b) % 2
            shift = sum(1 for r in removed if r < at)
            removed.append(at)
            steps.append((axis, axis, 1 << b, bit, at - shift))
        data = halve(data, steps)
        for b in range(1, dp_bits):
            got = exchange(data, "dp", 1 << b)
            low = (dp_i >> b) % 2 == 0
            data = jnp.where(low, jnp.concatenate([data, got], 0), jnp.concatenate([got, data], 0))
        pieces.append(data)
    part = jnp.concatenate(pieces, axis=1)
    back = exchange(part, "dp", 1)
    low = core == 0
    result = jnp.where(low, jnp.concatenate([part, back], 1), jnp.concatenate([back, part], 1))
    return result.astype(jnp.float32)


def body(layer_input, w_query, w_key, w_value, w_out, offsets, grad_out):
    rows = layer_input[0]
    cot = grad_out[0]
    tok = rows.shape[0]
    width = rows.shape[1]
    head = width // HEADS
    levels = lax.axis_size("seq").bit_length() - 1
    query = jnp.dot(rows, w_query, preferred_element_type=jnp.float32).astype(jnp.bfloat16)
    keys_local = jnp.dot(rows, w_key, preferred_element_type=jnp.float32).astype(jnp.bfloat16)
    values_local = jnp.dot(rows, w_value, preferred_element_type=jnp.float32).astype(jnp.bfloat16)
    remote = swap_blocks(keys_local, values_local, offsets, levels)
    all_keys = jnp.concatenate([keys_local] + [piece[0] for piece in remote], 0)
    all_values = jnp.concatenate([values_local] + [piece[1] for piece in remote], 0)
    d_att = jnp.dot(cot, w_out.T, preferred_element_type=jnp.float32).astype(jnp.bfloat16)
    attended, dquery, dk_acc, dv_acc = attention(query, all_keys, all_values, d_att, head)
    result = jnp.dot(attended, w_out, preferred_element_type=jnp.float32).astype(jnp.bfloat16)
    dkey_sum = dk_acc[:tok]
    dvalue_sum = dv_acc[:tok]
    for level in range(levels):
        low = tok + level * BLOCK
        piece = jnp.stack([dk_acc[low : low + BLOCK], dv_acc[low : low + BLOCK]])
        returned = partner(piece.astype(jnp.bfloat16), "seq", level).astype(piece.dtype)
        start = offsets[level] * BLOCK
        dkey_sum = lax.dynamic_update_slice_in_dim(
            dkey_sum, lax.dynamic_slice_in_dim(dkey_sum, start, BLOCK, 0) + returned[0], start, 0
        )
        dvalue_sum = lax.dynamic_update_slice_in_dim(
            dvalue_sum,
            lax.dynamic_slice_in_dim(dvalue_sum, start, BLOCK, 0) + returned[1],
            start,
            0,
        )
    dkey = dkey_sum.astype(jnp.bfloat16)
    dvalue = dvalue_sum.astype(jnp.bfloat16)
    total = jnp.dot(dquery, w_query.T, preferred_element_type=jnp.float32)
    total = total + jnp.dot(dkey, w_key.T, preferred_element_type=jnp.float32)
    total = total + jnp.dot(dvalue, w_value.T, preferred_element_type=jnp.float32)
    grad_input = total.astype(jnp.bfloat16)
    sources = ((rows, dquery), (rows, dkey), (rows, dvalue), (attended, cot))
    summed = reduce_gradients(gradient_terms(sources))
    return (
        result[None],
        grad_input[None],
        summed[:, :width],
        summed[:, width : 2 * width],
        summed[:, 2 * width : 3 * width],
        summed[:, 3 * width :],
    )


def solution(mesh):
    return jax.shard_map(
        body,
        mesh=mesh,
        in_specs=(P("dp", "seq", None), P(), P(), P(), P(), P(), P("dp", "seq", None)),
        out_specs=(
            P("dp", "seq", None),
            P("dp", "seq", None),
            P("seq", None),
            P("seq", None),
            P("seq", None),
            P("seq", None),
        ),
        check_vma=False,
    )
```

```python
import functools

import jax
import jax.numpy as jnp
from jax import lax
from jax.experimental import pallas as pl
from jax.experimental.pallas import tpu as pltpu
from jax.sharding import PartitionSpec as P

HEADS = 16
BLOCK = 128
LANES = 128


def partner(array, axis, apart):
    return lax.ppermute(array, axis, [(i, i ^ 1 << apart) for i in range(lax.axis_size(axis))])


def swap_blocks(keys_local, values_local, offsets, levels):
    remote = []
    for level in range(levels):
        start = offsets[level] * BLOCK
        pair = jnp.stack(
            [
                lax.dynamic_slice_in_dim(keys_local, start, BLOCK, 0),
                lax.dynamic_slice_in_dim(values_local, start, BLOCK, 0),
            ]
        )
        remote.append(partner(pair, "seq", level))
    return remote


def attention_kernel(q_ref, k_ref, v_ref, do_ref, att_ref, dq_ref, dk_ref, dv_ref, *, head, scale):
    q = q_ref[...]
    k = k_ref[...]
    v = v_ref[...]
    do = do_ref[...]
    width = q.shape[1]
    lane = lax.broadcasted_iota(jnp.int32, (1, width), 1)
    outs = None
    for j in range(width // head):
        inside = (lane >= j * head) & (lane < (j + 1) * head)
        qm = jnp.where(inside, q * jnp.asarray(scale, q.dtype), jnp.zeros_like(q))
        dom = jnp.where(inside, do, jnp.zeros_like(do))
        s = lax.dot_general(qm, k, (((1,), (1,)), ((), ())), preferred_element_type=jnp.float32)
        top = jnp.max(s, axis=-1, keepdims=True)
        e = jnp.exp(s - top)
        p = e * (1.0 / jnp.sum(e, axis=-1, keepdims=True))
        pb = p.astype(jnp.bfloat16)
        a = jnp.dot(pb, v, preferred_element_type=jnp.float32)
        dp = lax.dot_general(dom, v, (((1,), (1,)), ((), ())), preferred_element_type=jnp.float32)
        delta = jnp.sum(p * dp, axis=-1, keepdims=True)
        ds = (p * (dp - delta) * scale).astype(jnp.bfloat16)
        dq = jnp.dot(ds, k, preferred_element_type=jnp.float32)
        dk = lax.dot_general(ds, q, (((0,), (0,)), ((), ())), preferred_element_type=jnp.float32)
        dv = lax.dot_general(pb, do, (((0,), (0,)), ((), ())), preferred_element_type=jnp.float32)
        if outs is None:
            outs = [a, dq, dk, dv]
        else:
            outs = [jnp.where(inside, new, old) for new, old in zip([a, dq, dk, dv], outs)]
    att_ref[...] = outs[0].astype(att_ref.dtype)
    dq_ref[...] = outs[1].astype(dq_ref.dtype)
    dk_ref[...] = outs[2]
    dv_ref[...] = outs[3]


def attention(query, keys, values, d_att, head):
    tok, width = query.shape
    total = keys.shape[0]
    steps = width // LANES
    qspec = pl.BlockSpec((tok, LANES), lambda i: (0, i))
    kspec = pl.BlockSpec((total, LANES), lambda i: (0, i))
    return pl.pallas_call(
        functools.partial(attention_kernel, head=head, scale=head ** -0.5),
        grid=(steps,),
        in_specs=[qspec, kspec, kspec, qspec],
        out_specs=[qspec, qspec, kspec, kspec],
        out_shape=[
            jax.ShapeDtypeStruct((tok, width), jnp.bfloat16),
            jax.ShapeDtypeStruct((tok, width), jnp.bfloat16),
            jax.ShapeDtypeStruct((total, width), jnp.float32),
            jax.ShapeDtypeStruct((total, width), jnp.float32),
        ],
        compiler_params=pltpu.CompilerParams(vmem_limit_bytes=60 * 1024 * 1024),
        cost_estimate=pl.CostEstimate(
            flops=12 * tok * total * width * (LANES // head),
            transcendentals=tok * total * (width // head),
            bytes_accessed=4 * tok * width + 12 * total * width,
        ),
    )(query, keys, values, d_att)


def exchange(array, axis, mask):
    return lax.ppermute(array, axis, [(i, i ^ mask) for i in range(lax.axis_size(axis))])


def add_bf16(a, b):
    return (a.astype(jnp.float32) + b.astype(jnp.float32)).astype(jnp.bfloat16)


def term(left, right, lo, hi):
    return jnp.dot(left.T, right[:, lo:hi], preferred_element_type=jnp.float32).astype(jnp.bfloat16)


def reduce_gradients(sources):
    n_dp = lax.axis_size("dp")
    n_seq = lax.axis_size("seq")
    seq_bits = n_seq.bit_length() - 1
    dp_bits = n_dp.bit_length() - 1
    width = sources[0][1].shape[1]
    rows = sources[0][0].shape[1]
    blk = rows // n_seq
    dp_i = lax.axis_index("dp")
    seq_i = lax.axis_index("seq")
    low = dp_i % 2 == 0

    def pick(a, b):
        return jnp.where(low, a, b)

    keep = [
        (sources[0][0], pick(sources[0][1], sources[2][1])),
        (pick(sources[1][0], sources[3][0]), pick(sources[1][1], sources[3][1])),
    ]
    send = [
        (sources[2][0], pick(sources[2][1], sources[0][1])),
        (pick(sources[3][0], sources[1][0]), pick(sources[3][1], sources[1][1])),
    ]
    dims = [("seq", 0)] + [("dp", b) for b in range(1, dp_bits)] + [("seq", b) for b in range(1, seq_bits)]
    first = dims[:3]
    n_parts = len(first)
    units = 2 * width // LANES
    cuts = [units * p // n_parts * LANES for p in range(n_parts + 1)]
    shape = [2] * seq_bits + [2] * (dp_bits - 1) + [blk >> (dp_bits - 1)]
    pieces = []
    for p in range(n_parts):
        order = first[p:] + first[:p] + dims[3:]
        datas = []
        spans = []
        for g in range(2):
            lo = max(cuts[p], g * width) - g * width
            hi = min(cuts[p + 1], (g + 1) * width) - g * width
            if hi > lo:
                spans.append((g, lo, hi))
        sends = [term(*send[g], lo, hi) for g, lo, hi in spans]
        keeps = [term(*keep[g], lo, hi) for g, lo, hi in spans]
        got = exchange(sends, "dp", 1)
        datas = [add_bf16(k, r).reshape(shape + [k.shape[1]]) for k, r in zip(keeps, got)]
        removed = []
        for axis, b in order:
            if axis == "seq":
                at = seq_bits - 1 - b
                bit = (seq_i >> b) % 2
            else:
                at = seq_bits + (dp_bits - 1 - b)
                bit = (dp_i >> b) % 2
            at_now = at - sum(1 for r in removed if r < at)
            removed.append(at)
            kept = [lax.dynamic_index_in_dim(d, bit, at_now, keepdims=False) for d in datas]
            out = [lax.dynamic_index_in_dim(d, 1 - bit, at_now, keepdims=False) for d in datas]
            datas = [add_bf16(k, r) for k, r in zip(kept, exchange(out, axis, 1 << b))]
        for b in range(1, dp_bits):
            got = exchange(datas, "dp", 1 << b)
            first_half = (dp_i >> b) % 2 == 0
            datas = [
                jnp.where(first_half, jnp.concatenate([d, r], 0), jnp.concatenate([r, d], 0))
                for d, r in zip(datas, got)
            ]
        pieces.extend(datas)
    part = jnp.concatenate(pieces, axis=1)
    back = exchange(part, "dp", 1)
    mine = [part[:, :width], part[:, width:]]
    other = [back[:, :width], back[:, width:]]
    return (
        pick(mine[0], other[0]).astype(jnp.float32),
        pick(mine[1], other[1]).astype(jnp.float32),
        pick(other[0], mine[0]).astype(jnp.float32),
        pick(other[1], mine[1]).astype(jnp.float32),
    )


def body(layer_input, w_query, w_key, w_value, w_out, offsets, grad_out):
    rows = layer_input[0]
    cot = grad_out[0]
    tok = rows.shape[0]
    width = rows.shape[1]
    head = width // HEADS
    levels = lax.axis_size("seq").bit_length() - 1
    query = jnp.dot(rows, w_query, preferred_element_type=jnp.float32).astype(jnp.bfloat16)
    keys_local = jnp.dot(rows, w_key, preferred_element_type=jnp.float32).astype(jnp.bfloat16)
    values_local = jnp.dot(rows, w_value, preferred_element_type=jnp.float32).astype(jnp.bfloat16)
    remote = swap_blocks(keys_local, values_local, offsets, levels)
    all_keys = jnp.concatenate([keys_local] + [piece[0] for piece in remote], 0)
    all_values = jnp.concatenate([values_local] + [piece[1] for piece in remote], 0)
    d_att = jnp.dot(cot, w_out.T, preferred_element_type=jnp.float32).astype(jnp.bfloat16)
    attended, dquery, dk_acc, dv_acc = attention(query, all_keys, all_values, d_att, head)
    result = jnp.dot(attended, w_out, preferred_element_type=jnp.float32).astype(jnp.bfloat16)
    dkey_sum = dk_acc[:tok]
    dvalue_sum = dv_acc[:tok]
    for level in range(levels):
        low = tok + level * BLOCK
        piece = jnp.stack([dk_acc[low : low + BLOCK], dv_acc[low : low + BLOCK]])
        returned = partner(piece.astype(jnp.bfloat16), "seq", level).astype(piece.dtype)
        start = offsets[level] * BLOCK
        dkey_sum = lax.dynamic_update_slice_in_dim(
            dkey_sum, lax.dynamic_slice_in_dim(dkey_sum, start, BLOCK, 0) + returned[0], start, 0
        )
        dvalue_sum = lax.dynamic_update_slice_in_dim(
            dvalue_sum,
            lax.dynamic_slice_in_dim(dvalue_sum, start, BLOCK, 0) + returned[1],
            start,
            0,
        )
    dkey = dkey_sum.astype(jnp.bfloat16)
    dvalue = dvalue_sum.astype(jnp.bfloat16)
    total = jnp.dot(dquery, w_query.T, preferred_element_type=jnp.float32)
    total = total + jnp.dot(dkey, w_key.T, preferred_element_type=jnp.float32)
    total = total + jnp.dot(dvalue, w_value.T, preferred_element_type=jnp.float32)
    grad_input = total.astype(jnp.bfloat16)
    sources = ((rows, dquery), (rows, dkey), (rows, dvalue), (attended, cot))
    grads = reduce_gradients(sources)
    return (result[None], grad_input[None]) + grads


def solution(mesh):
    return jax.shard_map(
        body,
        mesh=mesh,
        in_specs=(P("dp", "seq", None), P(), P(), P(), P(), P(), P("dp", "seq", None)),
        out_specs=(
            P("dp", "seq", None),
            P("dp", "seq", None),
            P("seq", None),
            P("seq", None),
            P("seq", None),
            P("seq", None),
        ),
        check_vma=False,
    )
```

```python
import functools

import jax
import jax.numpy as jnp
from jax import lax
from jax.experimental import pallas as pl
from jax.experimental.pallas import tpu as pltpu
from jax.sharding import PartitionSpec as P

HEADS = 16
BLOCK = 128
LANES = 128


def partner(array, axis, apart):
    return lax.ppermute(array, axis, [(i, i ^ 1 << apart) for i in range(lax.axis_size(axis))])


def swap_blocks(keys_local, values_local, offsets, levels):
    remote = []
    for level in range(levels):
        start = offsets[level] * BLOCK
        pair = jnp.stack(
            [
                lax.dynamic_slice_in_dim(keys_local, start, BLOCK, 0),
                lax.dynamic_slice_in_dim(values_local, start, BLOCK, 0),
            ]
        )
        remote.append(partner(pair, "seq", level))
    return remote


def attention_kernel(q_ref, k_ref, v_ref, do_ref, att_ref, dq_ref, dk_ref, dv_ref, *, head, scale):
    q = q_ref[...]
    k = k_ref[...]
    v = v_ref[...]
    do = do_ref[...]
    width = q.shape[1]
    lane = lax.broadcasted_iota(jnp.int32, (1, width), 1)
    outs = None
    for j in range(width // head):
        inside = (lane >= j * head) & (lane < (j + 1) * head)
        qm = jnp.where(inside, q * jnp.asarray(scale, q.dtype), jnp.zeros_like(q))
        dom = jnp.where(inside, do, jnp.zeros_like(do))
        s = lax.dot_general(qm, k, (((1,), (1,)), ((), ())), preferred_element_type=jnp.float32)
        top = jnp.max(s, axis=-1, keepdims=True)
        e = jnp.exp(s - top)
        p = e * (1.0 / jnp.sum(e, axis=-1, keepdims=True))
        pb = p.astype(jnp.bfloat16)
        a = jnp.dot(pb, v, preferred_element_type=jnp.float32)
        dp = lax.dot_general(dom, v, (((1,), (1,)), ((), ())), preferred_element_type=jnp.float32)
        delta = jnp.sum(p * dp, axis=-1, keepdims=True)
        ds = (p * (dp - delta) * scale).astype(jnp.bfloat16)
        dq = jnp.dot(ds, k, preferred_element_type=jnp.float32)
        dk = lax.dot_general(ds, q, (((0,), (0,)), ((), ())), preferred_element_type=jnp.float32)
        dv = lax.dot_general(pb, do, (((0,), (0,)), ((), ())), preferred_element_type=jnp.float32)
        if outs is None:
            outs = [a, dq, dk, dv]
        else:
            outs = [jnp.where(inside, new, old) for new, old in zip([a, dq, dk, dv], outs)]
    att_ref[...] = outs[0].astype(att_ref.dtype)
    dq_ref[...] = outs[1].astype(dq_ref.dtype)
    dk_ref[...] = outs[2]
    dv_ref[...] = outs[3]


def attention(query, keys, values, d_att, head):
    tok, width = query.shape
    total = keys.shape[0]
    steps = width // LANES
    qspec = pl.BlockSpec((tok, LANES), lambda i: (0, i))
    kspec = pl.BlockSpec((total, LANES), lambda i: (0, i))
    return pl.pallas_call(
        functools.partial(attention_kernel, head=head, scale=head ** -0.5),
        grid=(steps,),
        in_specs=[qspec, kspec, kspec, qspec],
        out_specs=[qspec, qspec, kspec, kspec],
        out_shape=[
            jax.ShapeDtypeStruct((tok, width), jnp.bfloat16),
            jax.ShapeDtypeStruct((tok, width), jnp.bfloat16),
            jax.ShapeDtypeStruct((total, width), jnp.float32),
            jax.ShapeDtypeStruct((total, width), jnp.float32),
        ],
        compiler_params=pltpu.CompilerParams(vmem_limit_bytes=60 * 1024 * 1024),
        cost_estimate=pl.CostEstimate(
            flops=12 * tok * total * width * (LANES // head),
            transcendentals=tok * total * (width // head),
            bytes_accessed=4 * tok * width + 12 * total * width,
        ),
    )(query, keys, values, d_att)


def exchange(array, axis, mask):
    return lax.ppermute(array, axis, [(i, i ^ mask) for i in range(lax.axis_size(axis))])


def add_bf16(a, b):
    return (a.astype(jnp.float32) + b.astype(jnp.float32)).astype(jnp.bfloat16)


def term(left, right, lo, hi):
    return jnp.dot(left.T, right[:, lo:hi], preferred_element_type=jnp.float32).astype(jnp.bfloat16)


def reduce_gradients(sources):
    n_dp = lax.axis_size("dp")
    n_seq = lax.axis_size("seq")
    seq_bits = n_seq.bit_length() - 1
    dp_bits = n_dp.bit_length() - 1
    width = sources[0][1].shape[1]
    rows = sources[0][0].shape[1]
    blk = rows // n_seq
    dp_i = lax.axis_index("dp")
    seq_i = lax.axis_index("seq")
    low = dp_i % 2 == 0

    def pick(a, b):
        return jnp.where(low, a, b)

    keep = [
        (sources[0][0], pick(sources[0][1], sources[2][1])),
        (pick(sources[1][0], sources[3][0]), pick(sources[1][1], sources[3][1])),
    ]
    send = [
        (sources[2][0], pick(sources[2][1], sources[0][1])),
        (pick(sources[3][0], sources[1][0]), pick(sources[3][1], sources[1][1])),
    ]
    seq_dims = [("seq", b) for b in range(seq_bits)]
    dp_dims = [("dp", b) for b in range(1, dp_bits)]
    if seq_bits >= 2:
        orders = [
            seq_dims[:2] + dp_dims + seq_dims[2:],
            seq_dims[1::-1] + seq_dims[2:] + dp_dims,
        ]
    else:
        orders = [seq_dims + dp_dims] * 2
    shape = [2] * seq_bits + [2] * (dp_bits - 1) + [blk >> (dp_bits - 1)]
    sends = [term(*send[g], 0, width) for g in range(2)]
    keeps = [term(*keep[g], 0, width) for g in range(2)]
    got = exchange(sends, "dp", 1)
    pieces = []
    for g in range(2):
        data = add_bf16(keeps[g], got[g]).reshape(shape + [width])
        removed = []
        for axis, b in orders[g]:
            if axis == "seq":
                at = seq_bits - 1 - b
                bit = (seq_i >> b) % 2
            else:
                at = seq_bits + (dp_bits - 1 - b)
                bit = (dp_i >> b) % 2
            at_now = at - sum(1 for r in removed if r < at)
            removed.append(at)
            kept = lax.dynamic_index_in_dim(data, bit, at_now, keepdims=False)
            out = lax.dynamic_index_in_dim(data, 1 - bit, at_now, keepdims=False)
            data = add_bf16(kept, exchange(out, axis, 1 << b))
        pieces.append(data)
    data = jnp.concatenate(pieces, axis=1)
    for b in range(1, dp_bits):
        recv = exchange(data, "dp", 1 << b)
        first_half = (dp_i >> b) % 2 == 0
        data = jnp.where(first_half, jnp.concatenate([data, recv], 0), jnp.concatenate([recv, data], 0))
    pieces = [data]
    part = jnp.concatenate(pieces, axis=1)
    back = exchange(part, "dp", 1)
    mine = [part[:, :width], part[:, width:]]
    other = [back[:, :width], back[:, width:]]
    return (
        pick(mine[0], other[0]).astype(jnp.float32),
        pick(mine[1], other[1]).astype(jnp.float32),
        pick(other[0], mine[0]).astype(jnp.float32),
        pick(other[1], mine[1]).astype(jnp.float32),
    )


def body(layer_input, w_query, w_key, w_value, w_out, offsets, grad_out):
    rows = layer_input[0]
    cot = grad_out[0]
    tok = rows.shape[0]
    width = rows.shape[1]
    head = width // HEADS
    levels = lax.axis_size("seq").bit_length() - 1
    query = jnp.dot(rows, w_query, preferred_element_type=jnp.float32).astype(jnp.bfloat16)
    keys_local = jnp.dot(rows, w_key, preferred_element_type=jnp.float32).astype(jnp.bfloat16)
    values_local = jnp.dot(rows, w_value, preferred_element_type=jnp.float32).astype(jnp.bfloat16)
    remote = swap_blocks(keys_local, values_local, offsets, levels)
    all_keys = jnp.concatenate([keys_local] + [piece[0] for piece in remote], 0)
    all_values = jnp.concatenate([values_local] + [piece[1] for piece in remote], 0)
    d_att = jnp.dot(cot, w_out.T, preferred_element_type=jnp.float32).astype(jnp.bfloat16)
    attended, dquery, dk_acc, dv_acc = attention(query, all_keys, all_values, d_att, head)
    result = jnp.dot(attended, w_out, preferred_element_type=jnp.float32).astype(jnp.bfloat16)
    dkey_sum = dk_acc[:tok]
    dvalue_sum = dv_acc[:tok]
    for level in range(levels):
        low = tok + level * BLOCK
        piece = jnp.stack([dk_acc[low : low + BLOCK], dv_acc[low : low + BLOCK]])
        returned = partner(piece.astype(jnp.bfloat16), "seq", level).astype(piece.dtype)
        start = offsets[level] * BLOCK
        dkey_sum = lax.dynamic_update_slice_in_dim(
            dkey_sum, lax.dynamic_slice_in_dim(dkey_sum, start, BLOCK, 0) + returned[0], start, 0
        )
        dvalue_sum = lax.dynamic_update_slice_in_dim(
            dvalue_sum,
            lax.dynamic_slice_in_dim(dvalue_sum, start, BLOCK, 0) + returned[1],
            start,
            0,
        )
    dkey = dkey_sum.astype(jnp.bfloat16)
    dvalue = dvalue_sum.astype(jnp.bfloat16)
    total = jnp.dot(dquery, w_query.T, preferred_element_type=jnp.float32)
    total = total + jnp.dot(dkey, w_key.T, preferred_element_type=jnp.float32)
    total = total + jnp.dot(dvalue, w_value.T, preferred_element_type=jnp.float32)
    grad_input = total.astype(jnp.bfloat16)
    sources = ((rows, dquery), (rows, dkey), (rows, dvalue), (attended, cot))
    grads = reduce_gradients(sources)
    return (result[None], grad_input[None]) + grads


def solution(mesh):
    return jax.shard_map(
        body,
        mesh=mesh,
        in_specs=(P("dp", "seq", None), P(), P(), P(), P(), P(), P("dp", "seq", None)),
        out_specs=(
            P("dp", "seq", None),
            P("dp", "seq", None),
            P("seq", None),
            P("seq", None),
            P("seq", None),
            P("seq", None),
        ),
        check_vma=False,
    )
```

```python
import functools

import jax
import jax.numpy as jnp
from jax import lax
from jax.experimental import pallas as pl
from jax.experimental.pallas import tpu as pltpu
from jax.sharding import PartitionSpec as P

HEADS = 16
BLOCK = 128
LANES = 128


def partner(array, axis, apart):
    return lax.ppermute(array, axis, [(i, i ^ 1 << apart) for i in range(lax.axis_size(axis))])


def swap_blocks(keys_local, values_local, offsets, levels):
    remote = []
    for level in range(levels):
        start = offsets[level] * BLOCK
        pair = jnp.stack(
            [
                lax.dynamic_slice_in_dim(keys_local, start, BLOCK, 0),
                lax.dynamic_slice_in_dim(values_local, start, BLOCK, 0),
            ]
        )
        remote.append(partner(pair, "seq", level))
    return remote


def attention_kernel(q_ref, k_ref, v_ref, do_ref, att_ref, dq_ref, dk_ref, dv_ref, *, head, scale):
    q = q_ref[...]
    k = k_ref[...]
    v = v_ref[...]
    do = do_ref[...]
    width = q.shape[1]
    lane = lax.broadcasted_iota(jnp.int32, (1, width), 1)
    outs = None
    for j in range(width // head):
        inside = (lane >= j * head) & (lane < (j + 1) * head)
        qm = jnp.where(inside, q * jnp.asarray(scale, q.dtype), jnp.zeros_like(q))
        dom = jnp.where(inside, do, jnp.zeros_like(do))
        s = lax.dot_general(qm, k, (((1,), (1,)), ((), ())), preferred_element_type=jnp.float32)
        top = jnp.max(s, axis=-1, keepdims=True)
        e = jnp.exp(s - top)
        p = e * (1.0 / jnp.sum(e, axis=-1, keepdims=True))
        pb = p.astype(jnp.bfloat16)
        a = jnp.dot(pb, v, preferred_element_type=jnp.float32)
        dp = lax.dot_general(dom, v, (((1,), (1,)), ((), ())), preferred_element_type=jnp.float32)
        delta = jnp.sum(p * dp, axis=-1, keepdims=True)
        ds = (p * (dp - delta) * scale).astype(jnp.bfloat16)
        dq = jnp.dot(ds, k, preferred_element_type=jnp.float32)
        dk = lax.dot_general(ds, q, (((0,), (0,)), ((), ())), preferred_element_type=jnp.float32)
        dv = lax.dot_general(pb, do, (((0,), (0,)), ((), ())), preferred_element_type=jnp.float32)
        if outs is None:
            outs = [a, dq, dk, dv]
        else:
            outs = [jnp.where(inside, new, old) for new, old in zip([a, dq, dk, dv], outs)]
    att_ref[...] = outs[0].astype(att_ref.dtype)
    dq_ref[...] = outs[1].astype(dq_ref.dtype)
    dk_ref[...] = outs[2]
    dv_ref[...] = outs[3]


def attention(query, keys, values, d_att, head):
    tok, width = query.shape
    total = keys.shape[0]
    steps = width // LANES
    qspec = pl.BlockSpec((tok, LANES), lambda i: (0, i))
    kspec = pl.BlockSpec((total, LANES), lambda i: (0, i))
    return pl.pallas_call(
        functools.partial(attention_kernel, head=head, scale=head ** -0.5),
        grid=(steps,),
        in_specs=[qspec, kspec, kspec, qspec],
        out_specs=[qspec, qspec, kspec, kspec],
        out_shape=[
            jax.ShapeDtypeStruct((tok, width), jnp.bfloat16),
            jax.ShapeDtypeStruct((tok, width), jnp.bfloat16),
            jax.ShapeDtypeStruct((total, width), jnp.float32),
            jax.ShapeDtypeStruct((total, width), jnp.float32),
        ],
        compiler_params=pltpu.CompilerParams(vmem_limit_bytes=60 * 1024 * 1024),
        cost_estimate=pl.CostEstimate(
            flops=12 * tok * total * width * (LANES // head),
            transcendentals=tok * total * (width // head),
            bytes_accessed=4 * tok * width + 12 * total * width,
        ),
    )(query, keys, values, d_att)


def exchange(array, axis, mask):
    return lax.ppermute(array, axis, [(i, i ^ mask) for i in range(lax.axis_size(axis))])


def add_bf16(a, b):
    return (a.astype(jnp.float32) + b.astype(jnp.float32)).astype(jnp.bfloat16)


def term(left, right, lo, hi):
    return jnp.dot(left.T, right[:, lo:hi], preferred_element_type=jnp.float32).astype(jnp.bfloat16)


def halving_orders(seq_bits, dp_bits):
    seq_dims = [("seq", b) for b in range(seq_bits)]
    dp_dims = [("dp", b) for b in range(1, dp_bits)]
    if seq_bits >= 2:
        return [seq_dims[:2] + dp_dims + seq_dims[2:], seq_dims[1::-1] + seq_dims[2:] + dp_dims]
    return [seq_dims + dp_dims] * 2


def reduce_pair(first, second):
    n_dp = lax.axis_size("dp")
    n_seq = lax.axis_size("seq")
    seq_bits = n_seq.bit_length() - 1
    dp_bits = n_dp.bit_length() - 1
    width = first[1].shape[1]
    rows = first[0].shape[1]
    blk = rows // n_seq
    dp_i = lax.axis_index("dp")
    seq_i = lax.axis_index("seq")
    low = dp_i % 2 == 0
    keep = (jnp.where(low, first[0], second[0]), jnp.where(low, first[1], second[1]))
    send = (jnp.where(low, second[0], first[0]), jnp.where(low, second[1], first[1]))
    got = exchange(term(*send, 0, width), "dp", 1)
    shape = [2] * seq_bits + [2] * (dp_bits - 1) + [blk >> (dp_bits - 1)]
    cut = (width // LANES) // 2 * LANES
    spans = [(0, cut), (cut, width)]
    pieces = []
    for order, (lo, hi) in zip(halving_orders(seq_bits, dp_bits), spans):
        data = add_bf16(term(*keep, lo, hi), got[:, lo:hi]).reshape(shape + [hi - lo])
        removed = []
        for axis, b in order:
            if axis == "seq":
                at = seq_bits - 1 - b
                bit = (seq_i >> b) % 2
            else:
                at = seq_bits + (dp_bits - 1 - b)
                bit = (dp_i >> b) % 2
            at_now = at - sum(1 for r in removed if r < at)
            removed.append(at)
            kept = lax.dynamic_index_in_dim(data, bit, at_now, keepdims=False)
            out = lax.dynamic_index_in_dim(data, 1 - bit, at_now, keepdims=False)
            data = add_bf16(kept, exchange(out, axis, 1 << b))
        pieces.append(data)
    data = jnp.concatenate(pieces, axis=1)
    for b in range(1, dp_bits):
        recv = exchange(data, "dp", 1 << b)
        first_half = (dp_i >> b) % 2 == 0
        data = jnp.where(first_half, jnp.concatenate([data, recv], 0), jnp.concatenate([recv, data], 0))
    return data


def gather_pairs(early, late):
    width = early.shape[1]
    both = jnp.concatenate([early, late], axis=1)
    back = exchange(both, "dp", 1)
    low = lax.axis_index("dp") % 2 == 0
    mine = [both[:, :width], both[:, width:]]
    other = [back[:, :width], back[:, width:]]
    query = jnp.where(low, mine[0], other[0])
    outw = jnp.where(low, other[0], mine[0])
    key = jnp.where(low, mine[1], other[1])
    value = jnp.where(low, other[1], mine[1])
    return tuple(g.astype(jnp.float32) for g in (query, key, value, outw))


def body(layer_input, w_query, w_key, w_value, w_out, offsets, grad_out):
    rows = layer_input[0]
    cot = grad_out[0]
    tok = rows.shape[0]
    width = rows.shape[1]
    head = width // HEADS
    levels = lax.axis_size("seq").bit_length() - 1
    query = jnp.dot(rows, w_query, preferred_element_type=jnp.float32).astype(jnp.bfloat16)
    keys_local = jnp.dot(rows, w_key, preferred_element_type=jnp.float32).astype(jnp.bfloat16)
    values_local = jnp.dot(rows, w_value, preferred_element_type=jnp.float32).astype(jnp.bfloat16)
    remote = swap_blocks(keys_local, values_local, offsets, levels)
    all_keys = jnp.concatenate([keys_local] + [piece[0] for piece in remote], 0)
    all_values = jnp.concatenate([values_local] + [piece[1] for piece in remote], 0)
    d_att = jnp.dot(cot, w_out.T, preferred_element_type=jnp.float32).astype(jnp.bfloat16)
    attended, dquery, dk_acc, dv_acc = attention(query, all_keys, all_values, d_att, head)
    result = jnp.dot(attended, w_out, preferred_element_type=jnp.float32).astype(jnp.bfloat16)
    dkey_sum = dk_acc[:tok]
    dvalue_sum = dv_acc[:tok]
    for level in range(levels):
        low = tok + level * BLOCK
        piece = jnp.stack([dk_acc[low : low + BLOCK], dv_acc[low : low + BLOCK]])
        returned = partner(piece.astype(jnp.bfloat16), "seq", level).astype(piece.dtype)
        start = offsets[level] * BLOCK
        dkey_sum = lax.dynamic_update_slice_in_dim(
            dkey_sum, lax.dynamic_slice_in_dim(dkey_sum, start, BLOCK, 0) + returned[0], start, 0
        )
        dvalue_sum = lax.dynamic_update_slice_in_dim(
            dvalue_sum,
            lax.dynamic_slice_in_dim(dvalue_sum, start, BLOCK, 0) + returned[1],
            start,
            0,
        )
    dkey = dkey_sum.astype(jnp.bfloat16)
    dvalue = dvalue_sum.astype(jnp.bfloat16)
    total = jnp.dot(dquery, w_query.T, preferred_element_type=jnp.float32)
    total = total + jnp.dot(dkey, w_key.T, preferred_element_type=jnp.float32)
    total = total + jnp.dot(dvalue, w_value.T, preferred_element_type=jnp.float32)
    grad_input = total.astype(jnp.bfloat16)
    early = reduce_pair((rows, dquery), (attended, cot))
    late = reduce_pair((rows, dkey), (rows, dvalue))
    grads = gather_pairs(early, late)
    return (result[None], grad_input[None]) + grads


def solution(mesh):
    return jax.shard_map(
        body,
        mesh=mesh,
        in_specs=(P("dp", "seq", None), P(), P(), P(), P(), P(), P("dp", "seq", None)),
        out_specs=(
            P("dp", "seq", None),
            P("dp", "seq", None),
            P("seq", None),
            P("seq", None),
            P("seq", None),
            P("seq", None),
        ),
        check_vma=False,
    )
```

```python
import functools

import jax
import jax.numpy as jnp
from jax import lax
from jax.experimental import pallas as pl
from jax.experimental.pallas import tpu as pltpu
from jax.sharding import PartitionSpec as P

HEADS = 16
BLOCK = 128
LANES = 128


def partner(array, axis, apart):
    return lax.ppermute(array, axis, [(i, i ^ 1 << apart) for i in range(lax.axis_size(axis))])


def swap_blocks(rows, w_key, w_value, offsets, levels):
    remote = []
    for level in range(levels):
        block = lax.dynamic_slice_in_dim(rows, offsets[level] * BLOCK, BLOCK, 0)
        pair = jnp.stack(
            [
                jnp.dot(block, w_key, preferred_element_type=jnp.float32).astype(jnp.bfloat16),
                jnp.dot(block, w_value, preferred_element_type=jnp.float32).astype(jnp.bfloat16),
            ]
        )
        remote.append(partner(pair, "seq", level))
    return remote


def attention_kernel(q_ref, k_ref, v_ref, do_ref, *refs, head, scale):
    remote = refs[:-4]
    att_ref, dq_ref, dk_ref, dv_ref = refs[-4:]
    q = q_ref[...]
    k = jnp.concatenate([k_ref[...]] + [r[0] for r in remote], axis=0)
    v = jnp.concatenate([v_ref[...]] + [r[1] for r in remote], axis=0)
    do = do_ref[...]
    width = q.shape[1]
    lane = lax.broadcasted_iota(jnp.int32, (1, width), 1)
    outs = None
    for j in range(width // head):
        inside = (lane >= j * head) & (lane < (j + 1) * head)
        qm = jnp.where(inside, q * jnp.asarray(scale, q.dtype), jnp.zeros_like(q))
        dom = jnp.where(inside, do, jnp.zeros_like(do))
        s = lax.dot_general(qm, k, (((1,), (1,)), ((), ())), preferred_element_type=jnp.float32)
        top = jnp.max(s, axis=-1, keepdims=True)
        e = jnp.exp(s - top)
        p = e * (1.0 / jnp.sum(e, axis=-1, keepdims=True))
        pb = p.astype(jnp.bfloat16)
        a = jnp.dot(pb, v, preferred_element_type=jnp.float32)
        dp = lax.dot_general(dom, v, (((1,), (1,)), ((), ())), preferred_element_type=jnp.float32)
        delta = jnp.sum(p * dp, axis=-1, keepdims=True)
        ds = (p * (dp - delta) * scale).astype(jnp.bfloat16)
        dq = jnp.dot(ds, k, preferred_element_type=jnp.float32)
        dk = lax.dot_general(ds, q, (((0,), (0,)), ((), ())), preferred_element_type=jnp.float32)
        dv = lax.dot_general(pb, do, (((0,), (0,)), ((), ())), preferred_element_type=jnp.float32)
        if outs is None:
            outs = [a, dq, dk, dv]
        else:
            outs = [jnp.where(inside, new, old) for new, old in zip([a, dq, dk, dv], outs)]
    att_ref[...] = outs[0].astype(att_ref.dtype)
    dq_ref[...] = outs[1].astype(dq_ref.dtype)
    dk_ref[...] = outs[2]
    dv_ref[...] = outs[3]


def attention(query, keys, values, d_att, remote, head):
    tok, width = query.shape
    total = tok + sum(r.shape[1] for r in remote)
    steps = width // LANES
    qspec = pl.BlockSpec((tok, LANES), lambda i: (0, i))
    kspec = pl.BlockSpec((total, LANES), lambda i: (0, i))
    rspecs = [pl.BlockSpec((2, r.shape[1], LANES), lambda i: (0, 0, i)) for r in remote]
    return pl.pallas_call(
        functools.partial(attention_kernel, head=head, scale=head ** -0.5),
        grid=(steps,),
        in_specs=[qspec, qspec, qspec, qspec] + rspecs,
        out_specs=[qspec, qspec, kspec, kspec],
        out_shape=[
            jax.ShapeDtypeStruct((tok, width), jnp.bfloat16),
            jax.ShapeDtypeStruct((tok, width), jnp.bfloat16),
            jax.ShapeDtypeStruct((total, width), jnp.float32),
            jax.ShapeDtypeStruct((total, width), jnp.float32),
        ],
        compiler_params=pltpu.CompilerParams(vmem_limit_bytes=60 * 1024 * 1024),
        cost_estimate=pl.CostEstimate(
            flops=12 * tok * total * width * (LANES // head),
            transcendentals=tok * total * (width // head),
            bytes_accessed=4 * tok * width + 12 * total * width,
        ),
    )(query, keys, values, d_att, *remote)


def exchange(array, axis, mask):
    return lax.ppermute(array, axis, [(i, i ^ mask) for i in range(lax.axis_size(axis))])


def add_bf16(a, b):
    return (a.astype(jnp.float32) + b.astype(jnp.float32)).astype(jnp.bfloat16)


def term(left, right, lo, hi):
    return jnp.dot(left.T, right[:, lo:hi], preferred_element_type=jnp.float32).astype(jnp.bfloat16)


def reduce_gradients(sources):
    n_dp = lax.axis_size("dp")
    n_seq = lax.axis_size("seq")
    seq_bits = n_seq.bit_length() - 1
    dp_bits = n_dp.bit_length() - 1
    width = sources[0][1].shape[1]
    rows = sources[0][0].shape[1]
    blk = rows // n_seq
    dp_i = lax.axis_index("dp")
    seq_i = lax.axis_index("seq")
    low = dp_i % 2 == 0

    def pick(a, b):
        return jnp.where(low, a, b)

    keep = [
        (sources[0][0], pick(sources[0][1], sources[2][1])),
        (pick(sources[1][0], sources[3][0]), pick(sources[1][1], sources[3][1])),
    ]
    send = [
        (sources[2][0], pick(sources[2][1], sources[0][1])),
        (pick(sources[3][0], sources[1][0]), pick(sources[3][1], sources[1][1])),
    ]
    seq_dims = [("seq", b) for b in range(seq_bits)]
    dp_dims = [("dp", b) for b in range(1, dp_bits)]
    if seq_bits >= 2:
        orders = [
            seq_dims[:2] + dp_dims + seq_dims[2:],
            seq_dims[1::-1] + seq_dims[2:] + dp_dims,
        ]
    else:
        orders = [seq_dims + dp_dims] * 2
    shape = [2] * seq_bits + [2] * (dp_bits - 1) + [blk >> (dp_bits - 1)]
    sends = [term(*send[g], 0, width) for g in range(2)]
    keeps = [term(*keep[g], 0, width) for g in range(2)]
    got = exchange(sends, "dp", 1)
    pieces = []
    for g in range(2):
        data = add_bf16(keeps[g], got[g]).reshape(shape + [width])
        removed = []
        for axis, b in orders[g]:
            if axis == "seq":
                at = seq_bits - 1 - b
                bit = (seq_i >> b) % 2
            else:
                at = seq_bits + (dp_bits - 1 - b)
                bit = (dp_i >> b) % 2
            at_now = at - sum(1 for r in removed if r < at)
            removed.append(at)
            kept = lax.dynamic_index_in_dim(data, bit, at_now, keepdims=False)
            out = lax.dynamic_index_in_dim(data, 1 - bit, at_now, keepdims=False)
            data = add_bf16(kept, exchange(out, axis, 1 << b))
        pieces.append(data)
    data = jnp.concatenate(pieces, axis=1)
    for b in range(1, dp_bits):
        recv = exchange(data, "dp", 1 << b)
        first_half = (dp_i >> b) % 2 == 0
        data = jnp.where(first_half, jnp.concatenate([data, recv], 0), jnp.concatenate([recv, data], 0))
    pieces = [data]
    part = jnp.concatenate(pieces, axis=1)
    back = exchange(part, "dp", 1)
    mine = [part[:, :width], part[:, width:]]
    other = [back[:, :width], back[:, width:]]
    return (
        pick(mine[0], other[0]).astype(jnp.float32),
        pick(mine[1], other[1]).astype(jnp.float32),
        pick(other[0], mine[0]).astype(jnp.float32),
        pick(other[1], mine[1]).astype(jnp.float32),
    )


def body(layer_input, w_query, w_key, w_value, w_out, offsets, grad_out):
    rows = layer_input[0]
    cot = grad_out[0]
    tok = rows.shape[0]
    width = rows.shape[1]
    head = width // HEADS
    levels = lax.axis_size("seq").bit_length() - 1
    remote = swap_blocks(rows, w_key, w_value, offsets, levels)
    query = jnp.dot(rows, w_query, preferred_element_type=jnp.float32).astype(jnp.bfloat16)
    keys_local = jnp.dot(rows, w_key, preferred_element_type=jnp.float32).astype(jnp.bfloat16)
    values_local = jnp.dot(rows, w_value, preferred_element_type=jnp.float32).astype(jnp.bfloat16)
    d_att = jnp.dot(cot, w_out.T, preferred_element_type=jnp.float32).astype(jnp.bfloat16)
    attended, dquery, dk_acc, dv_acc = attention(query, keys_local, values_local, d_att, remote, head)
    result = jnp.dot(attended, w_out, preferred_element_type=jnp.float32).astype(jnp.bfloat16)
    dkey_sum = dk_acc[:tok]
    dvalue_sum = dv_acc[:tok]
    for level in range(levels):
        low = tok + level * BLOCK
        piece = jnp.stack([dk_acc[low : low + BLOCK], dv_acc[low : low + BLOCK]])
        returned = partner(piece.astype(jnp.bfloat16), "seq", level).astype(piece.dtype)
        start = offsets[level] * BLOCK
        dkey_sum = lax.dynamic_update_slice_in_dim(
            dkey_sum, lax.dynamic_slice_in_dim(dkey_sum, start, BLOCK, 0) + returned[0], start, 0
        )
        dvalue_sum = lax.dynamic_update_slice_in_dim(
            dvalue_sum,
            lax.dynamic_slice_in_dim(dvalue_sum, start, BLOCK, 0) + returned[1],
            start,
            0,
        )
    dkey = dkey_sum.astype(jnp.bfloat16)
    dvalue = dvalue_sum.astype(jnp.bfloat16)
    total = jnp.dot(dquery, w_query.T, preferred_element_type=jnp.float32)
    total = total + jnp.dot(dkey, w_key.T, preferred_element_type=jnp.float32)
    total = total + jnp.dot(dvalue, w_value.T, preferred_element_type=jnp.float32)
    grad_input = total.astype(jnp.bfloat16)
    sources = ((rows, dquery), (rows, dkey), (rows, dvalue), (attended, cot))
    grads = reduce_gradients(sources)
    return (result[None], grad_input[None]) + grads


def solution(mesh):
    return jax.shard_map(
        body,
        mesh=mesh,
        in_specs=(P("dp", "seq", None), P(), P(), P(), P(), P(), P("dp", "seq", None)),
        out_specs=(
            P("dp", "seq", None),
            P("dp", "seq", None),
            P("seq", None),
            P("seq", None),
            P("seq", None),
            P("seq", None),
        ),
        check_vma=False,
    )
```

```python
import functools

import jax
import jax.numpy as jnp
from jax import lax
from jax.experimental import pallas as pl
from jax.experimental.pallas import tpu as pltpu
from jax.sharding import PartitionSpec as P

HEADS = 16
BLOCK = 128
LANES = 128


def partner(array, axis, apart):
    return lax.ppermute(array, axis, [(i, i ^ 1 << apart) for i in range(lax.axis_size(axis))])


def swap_blocks(keys_local, values_local, offsets, levels):
    remote = []
    for level in range(levels):
        start = offsets[level] * BLOCK
        pair = jnp.stack(
            [
                lax.dynamic_slice_in_dim(keys_local, start, BLOCK, 0),
                lax.dynamic_slice_in_dim(values_local, start, BLOCK, 0),
            ]
        )
        remote.append(partner(pair, "seq", level))
    return remote


def attention_kernel(q_ref, k_ref, v_ref, do_ref, att_ref, dq_ref, dk_ref, dv_ref, *, head, scale):
    q = q_ref[...]
    k = k_ref[...]
    v = v_ref[...]
    do = do_ref[...]
    width = q.shape[1]
    lane = lax.broadcasted_iota(jnp.int32, (1, width), 1)
    row = lax.broadcasted_iota(jnp.int32, (width, 1), 0)
    q_t = q.T
    do_t = do.T
    outs = None
    for j in range(width // head):
        inside = (lane >= j * head) & (lane < (j + 1) * head)
        rows_in = (row >= j * head) & (row < (j + 1) * head)
        qm = jnp.where(inside, q * jnp.asarray(scale, q.dtype), jnp.zeros_like(q))
        dom = jnp.where(inside, do, jnp.zeros_like(do))
        s = lax.dot_general(qm, k, (((1,), (1,)), ((), ())), preferred_element_type=jnp.float32)
        top = jnp.max(s, axis=-1, keepdims=True)
        e = jnp.exp(s - top)
        p = e * (1.0 / jnp.sum(e, axis=-1, keepdims=True))
        pb = p.astype(jnp.bfloat16)
        a = jnp.dot(pb, v, preferred_element_type=jnp.float32)
        dp = lax.dot_general(dom, v, (((1,), (1,)), ((), ())), preferred_element_type=jnp.float32)
        delta = jnp.sum(p * dp, axis=-1, keepdims=True)
        ds = (p * (dp - delta) * scale).astype(jnp.bfloat16)
        dq = jnp.dot(ds, k, preferred_element_type=jnp.float32)
        dk_t = jnp.dot(q_t, ds, preferred_element_type=jnp.float32)
        dv_t = jnp.dot(do_t, pb, preferred_element_type=jnp.float32)
        if outs is None:
            outs = [a, dq, dk_t, dv_t]
        else:
            outs = [
                jnp.where(inside, a, outs[0]),
                jnp.where(inside, dq, outs[1]),
                jnp.where(rows_in, dk_t, outs[2]),
                jnp.where(rows_in, dv_t, outs[3]),
            ]
    att_ref[...] = outs[0].astype(att_ref.dtype)
    dq_ref[...] = outs[1].astype(dq_ref.dtype)
    dk_ref[...] = outs[2].T
    dv_ref[...] = outs[3].T


def attention(query, keys, values, d_att, head):
    tok, width = query.shape
    total = keys.shape[0]
    steps = width // LANES
    qspec = pl.BlockSpec((tok, LANES), lambda i: (0, i))
    kspec = pl.BlockSpec((total, LANES), lambda i: (0, i))
    return pl.pallas_call(
        functools.partial(attention_kernel, head=head, scale=head ** -0.5),
        grid=(steps,),
        in_specs=[qspec, kspec, kspec, qspec],
        out_specs=[qspec, qspec, kspec, kspec],
        out_shape=[
            jax.ShapeDtypeStruct((tok, width), jnp.bfloat16),
            jax.ShapeDtypeStruct((tok, width), jnp.bfloat16),
            jax.ShapeDtypeStruct((total, width), jnp.float32),
            jax.ShapeDtypeStruct((total, width), jnp.float32),
        ],
        compiler_params=pltpu.CompilerParams(vmem_limit_bytes=60 * 1024 * 1024),
        cost_estimate=pl.CostEstimate(
            flops=12 * tok * total * width * (LANES // head),
            transcendentals=tok * total * (width // head),
            bytes_accessed=4 * tok * width + 12 * total * width,
        ),
    )(query, keys, values, d_att)


def exchange(array, axis, mask):
    return lax.ppermute(array, axis, [(i, i ^ mask) for i in range(lax.axis_size(axis))])


def add_bf16(a, b):
    return (a.astype(jnp.float32) + b.astype(jnp.float32)).astype(jnp.bfloat16)


def term(left, right, lo, hi):
    return jnp.dot(left.T, right[:, lo:hi], preferred_element_type=jnp.float32).astype(jnp.bfloat16)


def reduce_gradients(sources):
    n_dp = lax.axis_size("dp")
    n_seq = lax.axis_size("seq")
    seq_bits = n_seq.bit_length() - 1
    dp_bits = n_dp.bit_length() - 1
    width = sources[0][1].shape[1]
    rows = sources[0][0].shape[1]
    blk = rows // n_seq
    dp_i = lax.axis_index("dp")
    seq_i = lax.axis_index("seq")
    low = dp_i % 2 == 0

    def pick(a, b):
        return jnp.where(low, a, b)

    keep = [
        (sources[0][0], pick(sources[0][1], sources[2][1])),
        (pick(sources[1][0], sources[3][0]), pick(sources[1][1], sources[3][1])),
    ]
    send = [
        (sources[2][0], pick(sources[2][1], sources[0][1])),
        (pick(sources[3][0], sources[1][0]), pick(sources[3][1], sources[1][1])),
    ]
    seq_dims = [("seq", b) for b in range(seq_bits)]
    dp_dims = [("dp", b) for b in range(1, dp_bits)]
    if seq_bits >= 2:
        orders = [
            seq_dims[:2] + dp_dims + seq_dims[2:],
            seq_dims[1::-1] + seq_dims[2:] + dp_dims,
        ]
    else:
        orders = [seq_dims + dp_dims] * 2
    shape = [2] * seq_bits + [2] * (dp_bits - 1) + [blk >> (dp_bits - 1)]
    sends = [term(*send[g], 0, width) for g in range(2)]
    keeps = [term(*keep[g], 0, width) for g in range(2)]
    got = exchange(sends, "dp", 1)
    pieces = []
    for g in range(2):
        data = add_bf16(keeps[g], got[g]).reshape(shape + [width])
        removed = []
        for axis, b in orders[g]:
            if axis == "seq":
                at = seq_bits - 1 - b
                bit = (seq_i >> b) % 2
            else:
                at = seq_bits + (dp_bits - 1 - b)
                bit = (dp_i >> b) % 2
            at_now = at - sum(1 for r in removed if r < at)
            removed.append(at)
            kept = lax.dynamic_index_in_dim(data, bit, at_now, keepdims=False)
            out = lax.dynamic_index_in_dim(data, 1 - bit, at_now, keepdims=False)
            data = add_bf16(kept, exchange(out, axis, 1 << b))
        pieces.append(data)
    data = jnp.concatenate(pieces, axis=1)
    for b in range(1, dp_bits):
        recv = exchange(data, "dp", 1 << b)
        first_half = (dp_i >> b) % 2 == 0
        data = jnp.where(first_half, jnp.concatenate([data, recv], 0), jnp.concatenate([recv, data], 0))
    pieces = [data]
    part = jnp.concatenate(pieces, axis=1)
    back = exchange(part, "dp", 1)
    mine = [part[:, :width], part[:, width:]]
    other = [back[:, :width], back[:, width:]]
    return (
        pick(mine[0], other[0]).astype(jnp.float32),
        pick(mine[1], other[1]).astype(jnp.float32),
        pick(other[0], mine[0]).astype(jnp.float32),
        pick(other[1], mine[1]).astype(jnp.float32),
    )


def body(layer_input, w_query, w_key, w_value, w_out, offsets, grad_out):
    rows = layer_input[0]
    cot = grad_out[0]
    tok = rows.shape[0]
    width = rows.shape[1]
    head = width // HEADS
    levels = lax.axis_size("seq").bit_length() - 1
    query = jnp.dot(rows, w_query, preferred_element_type=jnp.float32).astype(jnp.bfloat16)
    keys_local = jnp.dot(rows, w_key, preferred_element_type=jnp.float32).astype(jnp.bfloat16)
    values_local = jnp.dot(rows, w_value, preferred_element_type=jnp.float32).astype(jnp.bfloat16)
    remote = swap_blocks(keys_local, values_local, offsets, levels)
    all_keys = jnp.concatenate([keys_local] + [piece[0] for piece in remote], 0)
    all_values = jnp.concatenate([values_local] + [piece[1] for piece in remote], 0)
    d_att = jnp.dot(cot, w_out.T, preferred_element_type=jnp.float32).astype(jnp.bfloat16)
    attended, dquery, dk_acc, dv_acc = attention(query, all_keys, all_values, d_att, head)
    result = jnp.dot(attended, w_out, preferred_element_type=jnp.float32).astype(jnp.bfloat16)
    dkey_sum = dk_acc[:tok]
    dvalue_sum = dv_acc[:tok]
    for level in range(levels):
        low = tok + level * BLOCK
        piece = jnp.stack([dk_acc[low : low + BLOCK], dv_acc[low : low + BLOCK]])
        returned = partner(piece.astype(jnp.bfloat16), "seq", level).astype(piece.dtype)
        start = offsets[level] * BLOCK
        dkey_sum = lax.dynamic_update_slice_in_dim(
            dkey_sum, lax.dynamic_slice_in_dim(dkey_sum, start, BLOCK, 0) + returned[0], start, 0
        )
        dvalue_sum = lax.dynamic_update_slice_in_dim(
            dvalue_sum,
            lax.dynamic_slice_in_dim(dvalue_sum, start, BLOCK, 0) + returned[1],
            start,
            0,
        )
    dkey = dkey_sum.astype(jnp.bfloat16)
    dvalue = dvalue_sum.astype(jnp.bfloat16)
    total = jnp.dot(dquery, w_query.T, preferred_element_type=jnp.float32)
    total = total + jnp.dot(dkey, w_key.T, preferred_element_type=jnp.float32)
    total = total + jnp.dot(dvalue, w_value.T, preferred_element_type=jnp.float32)
    grad_input = total.astype(jnp.bfloat16)
    sources = ((rows, dquery), (rows, dkey), (rows, dvalue), (attended, cot))
    grads = reduce_gradients(sources)
    return (result[None], grad_input[None]) + grads


def solution(mesh):
    return jax.shard_map(
        body,
        mesh=mesh,
        in_specs=(P("dp", "seq", None), P(), P(), P(), P(), P(), P("dp", "seq", None)),
        out_specs=(
            P("dp", "seq", None),
            P("dp", "seq", None),
            P("seq", None),
            P("seq", None),
            P("seq", None),
            P("seq", None),
        ),
        check_vma=False,
    )
```

```python
import functools

import jax
import jax.numpy as jnp
from jax import lax
from jax.experimental import pallas as pl
from jax.experimental.pallas import tpu as pltpu
from jax.sharding import PartitionSpec as P

HEADS = 16
BLOCK = 128
LANES = 128


def partner(array, axis, apart):
    return lax.ppermute(array, axis, [(i, i ^ 1 << apart) for i in range(lax.axis_size(axis))])


def swap_blocks(keys_local, values_local, offsets, levels):
    remote = []
    for level in range(levels):
        start = offsets[level] * BLOCK
        pair = jnp.stack(
            [
                lax.dynamic_slice_in_dim(keys_local, start, BLOCK, 0),
                lax.dynamic_slice_in_dim(values_local, start, BLOCK, 0),
            ]
        )
        remote.append(partner(pair, "seq", level))
    return remote


def attention_kernel(q_ref, k_ref, v_ref, do_ref, att_ref, dq_ref, dk_ref, dv_ref, *, head, scale):
    q = q_ref[...]
    k = k_ref[...]
    v = v_ref[...]
    do = do_ref[...]
    width = q.shape[1]
    lane = lax.broadcasted_iota(jnp.int32, (1, width), 1)
    row = lax.broadcasted_iota(jnp.int32, (width, 1), 0)
    q_t = q.T
    do_t = do.T
    probs, grads, v_parts, k_parts, q_parts, do_parts = [], [], [], [], [], []
    for j in range(width // head):
        inside = (lane >= j * head) & (lane < (j + 1) * head)
        rows_in = (row >= j * head) & (row < (j + 1) * head)
        qm = jnp.where(inside, q * jnp.asarray(scale, q.dtype), jnp.zeros_like(q))
        dom = jnp.where(inside, do, jnp.zeros_like(do))
        s = lax.dot_general(qm, k, (((1,), (1,)), ((), ())), preferred_element_type=jnp.float32)
        top = jnp.max(s, axis=-1, keepdims=True)
        e = jnp.exp(s - top)
        p = e * (1.0 / jnp.sum(e, axis=-1, keepdims=True))
        dp = lax.dot_general(dom, v, (((1,), (1,)), ((), ())), preferred_element_type=jnp.float32)
        delta = jnp.sum(p * dp, axis=-1, keepdims=True)
        probs.append(p.astype(jnp.bfloat16))
        grads.append((p * (dp - delta) * scale).astype(jnp.bfloat16))
        v_parts.append(jnp.where(inside, v, jnp.zeros_like(v)))
        k_parts.append(jnp.where(inside, k, jnp.zeros_like(k)))
        q_parts.append(jnp.where(rows_in, q_t, jnp.zeros_like(q_t)))
        do_parts.append(jnp.where(rows_in, do_t, jnp.zeros_like(do_t)))
    att = jnp.dot(jnp.concatenate(probs, 1), jnp.concatenate(v_parts, 0), preferred_element_type=jnp.float32)
    dq = jnp.dot(jnp.concatenate(grads, 1), jnp.concatenate(k_parts, 0), preferred_element_type=jnp.float32)
    dk_t = jnp.dot(jnp.concatenate(q_parts, 1), jnp.concatenate(grads, 0), preferred_element_type=jnp.float32)
    dv_t = jnp.dot(jnp.concatenate(do_parts, 1), jnp.concatenate(probs, 0), preferred_element_type=jnp.float32)
    att_ref[...] = att.astype(att_ref.dtype)
    dq_ref[...] = dq.astype(dq_ref.dtype)
    dk_ref[...] = dk_t.T
    dv_ref[...] = dv_t.T


def attention(query, keys, values, d_att, head):
    tok, width = query.shape
    total = keys.shape[0]
    steps = width // LANES
    qspec = pl.BlockSpec((tok, LANES), lambda i: (0, i))
    kspec = pl.BlockSpec((total, LANES), lambda i: (0, i))
    return pl.pallas_call(
        functools.partial(attention_kernel, head=head, scale=head ** -0.5),
        grid=(steps,),
        in_specs=[qspec, kspec, kspec, qspec],
        out_specs=[qspec, qspec, kspec, kspec],
        out_shape=[
            jax.ShapeDtypeStruct((tok, width), jnp.bfloat16),
            jax.ShapeDtypeStruct((tok, width), jnp.bfloat16),
            jax.ShapeDtypeStruct((total, width), jnp.float32),
            jax.ShapeDtypeStruct((total, width), jnp.float32),
        ],
        compiler_params=pltpu.CompilerParams(vmem_limit_bytes=60 * 1024 * 1024),
        cost_estimate=pl.CostEstimate(
            flops=12 * tok * total * width * (LANES // head),
            transcendentals=tok * total * (width // head),
            bytes_accessed=4 * tok * width + 12 * total * width,
        ),
    )(query, keys, values, d_att)


def exchange(array, axis, mask):
    return lax.ppermute(array, axis, [(i, i ^ mask) for i in range(lax.axis_size(axis))])


def add_bf16(a, b):
    return (a.astype(jnp.float32) + b.astype(jnp.float32)).astype(jnp.bfloat16)


def term(left, right, lo, hi):
    return jnp.dot(left.T, right[:, lo:hi], preferred_element_type=jnp.float32).astype(jnp.bfloat16)


def reduce_gradients(sources):
    n_dp = lax.axis_size("dp")
    n_seq = lax.axis_size("seq")
    seq_bits = n_seq.bit_length() - 1
    dp_bits = n_dp.bit_length() - 1
    width = sources[0][1].shape[1]
    rows = sources[0][0].shape[1]
    blk = rows // n_seq
    dp_i = lax.axis_index("dp")
    seq_i = lax.axis_index("seq")
    low = dp_i % 2 == 0

    def pick(a, b):
        return jnp.where(low, a, b)

    keep = [
        (sources[0][0], pick(sources[0][1], sources[2][1])),
        (pick(sources[1][0], sources[3][0]), pick(sources[1][1], sources[3][1])),
    ]
    send = [
        (sources[2][0], pick(sources[2][1], sources[0][1])),
        (pick(sources[3][0], sources[1][0]), pick(sources[3][1], sources[1][1])),
    ]
    seq_dims = [("seq", b) for b in range(seq_bits)]
    dp_dims = [("dp", b) for b in range(1, dp_bits)]
    if seq_bits >= 2:
        orders = [
            seq_dims[:2] + dp_dims + seq_dims[2:],
            seq_dims[1::-1] + seq_dims[2:] + dp_dims,
        ]
    else:
        orders = [seq_dims + dp_dims] * 2
    shape = [2] * seq_bits + [2] * (dp_bits - 1) + [blk >> (dp_bits - 1)]
    sends = [term(*send[g], 0, width) for g in range(2)]
    keeps = [term(*keep[g], 0, width) for g in range(2)]
    got = exchange(sends, "dp", 1)
    pieces = []
    for g in range(2):
        data = add_bf16(keeps[g], got[g]).reshape(shape + [width])
        removed = []
        for axis, b in orders[g]:
            if axis == "seq":
                at = seq_bits - 1 - b
                bit = (seq_i >> b) % 2
            else:
                at = seq_bits + (dp_bits - 1 - b)
                bit = (dp_i >> b) % 2
            at_now = at - sum(1 for r in removed if r < at)
            removed.append(at)
            kept = lax.dynamic_index_in_dim(data, bit, at_now, keepdims=False)
            out = lax.dynamic_index_in_dim(data, 1 - bit, at_now, keepdims=False)
            data = add_bf16(kept, exchange(out, axis, 1 << b))
        pieces.append(data)
    data = jnp.concatenate(pieces, axis=1)
    for b in range(1, dp_bits):
        recv = exchange(data, "dp", 1 << b)
        first_half = (dp_i >> b) % 2 == 0
        data = jnp.where(first_half, jnp.concatenate([data, recv], 0), jnp.concatenate([recv, data], 0))
    pieces = [data]
    part = jnp.concatenate(pieces, axis=1)
    back = exchange(part, "dp", 1)
    mine = [part[:, :width], part[:, width:]]
    other = [back[:, :width], back[:, width:]]
    return (
        pick(mine[0], other[0]).astype(jnp.float32),
        pick(mine[1], other[1]).astype(jnp.float32),
        pick(other[0], mine[0]).astype(jnp.float32),
        pick(other[1], mine[1]).astype(jnp.float32),
    )


def body(layer_input, w_query, w_key, w_value, w_out, offsets, grad_out):
    rows = layer_input[0]
    cot = grad_out[0]
    tok = rows.shape[0]
    width = rows.shape[1]
    head = width // HEADS
    levels = lax.axis_size("seq").bit_length() - 1
    query = jnp.dot(rows, w_query, preferred_element_type=jnp.float32).astype(jnp.bfloat16)
    keys_local = jnp.dot(rows, w_key, preferred_element_type=jnp.float32).astype(jnp.bfloat16)
    values_local = jnp.dot(rows, w_value, preferred_element_type=jnp.float32).astype(jnp.bfloat16)
    remote = swap_blocks(keys_local, values_local, offsets, levels)
    all_keys = jnp.concatenate([keys_local] + [piece[0] for piece in remote], 0)
    all_values = jnp.concatenate([values_local] + [piece[1] for piece in remote], 0)
    d_att = jnp.dot(cot, w_out.T, preferred_element_type=jnp.float32).astype(jnp.bfloat16)
    attended, dquery, dk_acc, dv_acc = attention(query, all_keys, all_values, d_att, head)
    result = jnp.dot(attended, w_out, preferred_element_type=jnp.float32).astype(jnp.bfloat16)
    dkey_sum = dk_acc[:tok]
    dvalue_sum = dv_acc[:tok]
    for level in range(levels):
        low = tok + level * BLOCK
        piece = jnp.stack([dk_acc[low : low + BLOCK], dv_acc[low : low + BLOCK]])
        returned = partner(piece.astype(jnp.bfloat16), "seq", level).astype(piece.dtype)
        start = offsets[level] * BLOCK
        dkey_sum = lax.dynamic_update_slice_in_dim(
            dkey_sum, lax.dynamic_slice_in_dim(dkey_sum, start, BLOCK, 0) + returned[0], start, 0
        )
        dvalue_sum = lax.dynamic_update_slice_in_dim(
            dvalue_sum,
            lax.dynamic_slice_in_dim(dvalue_sum, start, BLOCK, 0) + returned[1],
            start,
            0,
        )
    dkey = dkey_sum.astype(jnp.bfloat16)
    dvalue = dvalue_sum.astype(jnp.bfloat16)
    total = jnp.dot(dquery, w_query.T, preferred_element_type=jnp.float32)
    total = total + jnp.dot(dkey, w_key.T, preferred_element_type=jnp.float32)
    total = total + jnp.dot(dvalue, w_value.T, preferred_element_type=jnp.float32)
    grad_input = total.astype(jnp.bfloat16)
    sources = ((rows, dquery), (rows, dkey), (rows, dvalue), (attended, cot))
    grads = reduce_gradients(sources)
    return (result[None], grad_input[None]) + grads


def solution(mesh):
    return jax.shard_map(
        body,
        mesh=mesh,
        in_specs=(P("dp", "seq", None), P(), P(), P(), P(), P(), P("dp", "seq", None)),
        out_specs=(
            P("dp", "seq", None),
            P("dp", "seq", None),
            P("seq", None),
            P("seq", None),
            P("seq", None),
            P("seq", None),
        ),
        check_vma=False,
    )
```

```python
import functools

import jax
import jax.numpy as jnp
from jax import lax
from jax.experimental import pallas as pl
from jax.experimental.pallas import tpu as pltpu
from jax.sharding import PartitionSpec as P

HEADS = 16
BLOCK = 128
LANES = 128


def partner(array, axis, apart):
    return lax.ppermute(array, axis, [(i, i ^ 1 << apart) for i in range(lax.axis_size(axis))])


def swap_blocks(keys_local, values_local, offsets, levels):
    remote = []
    for level in range(levels):
        start = offsets[level] * BLOCK
        pair = jnp.stack(
            [
                lax.dynamic_slice_in_dim(keys_local, start, BLOCK, 0),
                lax.dynamic_slice_in_dim(values_local, start, BLOCK, 0),
            ]
        )
        remote.append(partner(pair, "seq", level))
    return remote


def attention_kernel(q_ref, k_ref, v_ref, do_ref, *refs, head, scale):
    remote = refs[:-5]
    att_ref, dq_ref, dk_ref, dv_ref, back_ref = refs[-5:]
    q = q_ref[...]
    k = jnp.concatenate([k_ref[...]] + [r[0] for r in remote], axis=0)
    v = jnp.concatenate([v_ref[...]] + [r[1] for r in remote], axis=0)
    do = do_ref[...]
    width = q.shape[1]
    lane = lax.broadcasted_iota(jnp.int32, (1, width), 1)
    row = lax.broadcasted_iota(jnp.int32, (width, 1), 0)
    q_t = q.T
    do_t = do.T
    probs, grads, v_parts, k_parts, q_parts, do_parts = [], [], [], [], [], []
    for j in range(width // head):
        inside = (lane >= j * head) & (lane < (j + 1) * head)
        rows_in = (row >= j * head) & (row < (j + 1) * head)
        qm = jnp.where(inside, q * jnp.asarray(scale, q.dtype), jnp.zeros_like(q))
        dom = jnp.where(inside, do, jnp.zeros_like(do))
        s = lax.dot_general(qm, k, (((1,), (1,)), ((), ())), preferred_element_type=jnp.float32)
        top = jnp.max(s, axis=-1, keepdims=True)
        e = jnp.exp(s - top)
        p = e * (1.0 / jnp.sum(e, axis=-1, keepdims=True))
        dp = lax.dot_general(dom, v, (((1,), (1,)), ((), ())), preferred_element_type=jnp.float32)
        delta = jnp.sum(p * dp, axis=-1, keepdims=True)
        probs.append(p.astype(jnp.bfloat16))
        grads.append((p * (dp - delta) * scale).astype(jnp.bfloat16))
        v_parts.append(jnp.where(inside, v, jnp.zeros_like(v)))
        k_parts.append(jnp.where(inside, k, jnp.zeros_like(k)))
        q_parts.append(jnp.where(rows_in, q_t, jnp.zeros_like(q_t)))
        do_parts.append(jnp.where(rows_in, do_t, jnp.zeros_like(do_t)))
    att = jnp.dot(jnp.concatenate(probs, 1), jnp.concatenate(v_parts, 0), preferred_element_type=jnp.float32)
    dq = jnp.dot(jnp.concatenate(grads, 1), jnp.concatenate(k_parts, 0), preferred_element_type=jnp.float32)
    dk_t = jnp.dot(jnp.concatenate(q_parts, 1), jnp.concatenate(grads, 0), preferred_element_type=jnp.float32)
    dv_t = jnp.dot(jnp.concatenate(do_parts, 1), jnp.concatenate(probs, 0), preferred_element_type=jnp.float32)
    att_ref[...] = att.astype(att_ref.dtype)
    dq_ref[...] = dq.astype(dq_ref.dtype)
    dk = dk_t.T
    dv = dv_t.T
    tok = q.shape[0]
    dk_ref[...] = dk[:tok]
    dv_ref[...] = dv[:tok]
    low = tok
    for level, r in enumerate(remote):
        high = low + r.shape[1]
        back_ref[level, 0] = dk[low:high].astype(back_ref.dtype)
        back_ref[level, 1] = dv[low:high].astype(back_ref.dtype)
        low = high


def attention(query, keys, values, d_att, remote, head):
    tok, width = query.shape
    levels = len(remote)
    block = remote[0].shape[1]
    total = tok + levels * block
    steps = width // LANES
    qspec = pl.BlockSpec((tok, LANES), lambda i: (0, i))
    rspec = pl.BlockSpec((2, block, LANES), lambda i: (0, 0, i))
    bspec = pl.BlockSpec((levels, 2, block, LANES), lambda i: (0, 0, 0, i))
    return pl.pallas_call(
        functools.partial(attention_kernel, head=head, scale=head ** -0.5),
        grid=(steps,),
        in_specs=[qspec] * 4 + [rspec] * levels,
        out_specs=[qspec] * 4 + [bspec],
        out_shape=[
            jax.ShapeDtypeStruct((tok, width), jnp.bfloat16),
            jax.ShapeDtypeStruct((tok, width), jnp.bfloat16),
            jax.ShapeDtypeStruct((tok, width), jnp.float32),
            jax.ShapeDtypeStruct((tok, width), jnp.float32),
            jax.ShapeDtypeStruct((levels, 2, block, width), jnp.bfloat16),
        ],
        compiler_params=pltpu.CompilerParams(vmem_limit_bytes=60 * 1024 * 1024),
        cost_estimate=pl.CostEstimate(
            flops=12 * tok * total * width * (LANES // head),
            transcendentals=tok * total * (width // head),
            bytes_accessed=4 * tok * width + 12 * total * width,
        ),
    )(query, keys, values, d_att, *remote)


def exchange(array, axis, mask):
    return lax.ppermute(array, axis, [(i, i ^ mask) for i in range(lax.axis_size(axis))])


def add_bf16(a, b):
    return (a.astype(jnp.float32) + b.astype(jnp.float32)).astype(jnp.bfloat16)


def term(left, right, lo, hi):
    return jnp.dot(left.T, right[:, lo:hi], preferred_element_type=jnp.float32).astype(jnp.bfloat16)


def reduce_gradients(sources):
    n_dp = lax.axis_size("dp")
    n_seq = lax.axis_size("seq")
    seq_bits = n_seq.bit_length() - 1
    dp_bits = n_dp.bit_length() - 1
    width = sources[0][1].shape[1]
    rows = sources[0][0].shape[1]
    blk = rows // n_seq
    dp_i = lax.axis_index("dp")
    seq_i = lax.axis_index("seq")
    low = dp_i % 2 == 0

    def pick(a, b):
        return jnp.where(low, a, b)

    keep = [
        (sources[0][0], pick(sources[0][1], sources[2][1])),
        (pick(sources[1][0], sources[3][0]), pick(sources[1][1], sources[3][1])),
    ]
    send = [
        (sources[2][0], pick(sources[2][1], sources[0][1])),
        (pick(sources[3][0], sources[1][0]), pick(sources[3][1], sources[1][1])),
    ]
    seq_dims = [("seq", b) for b in range(seq_bits)]
    dp_dims = [("dp", b) for b in range(1, dp_bits)]
    if seq_bits >= 2:
        orders = [
            seq_dims[:2] + dp_dims + seq_dims[2:],
            seq_dims[1::-1] + seq_dims[2:] + dp_dims,
        ]
    else:
        orders = [seq_dims + dp_dims] * 2
    shape = [2] * seq_bits + [2] * (dp_bits - 1) + [blk >> (dp_bits - 1)]
    sends = [term(*send[g], 0, width) for g in range(2)]
    keeps = [term(*keep[g], 0, width) for g in range(2)]
    got = exchange(sends, "dp", 1)
    pieces = []
    for g in range(2):
        data = add_bf16(keeps[g], got[g]).reshape(shape + [width])
        removed = []
        for axis, b in orders[g]:
            if axis == "seq":
                at = seq_bits - 1 - b
                bit = (seq_i >> b) % 2
            else:
                at = seq_bits + (dp_bits - 1 - b)
                bit = (dp_i >> b) % 2
            at_now = at - sum(1 for r in removed if r < at)
            removed.append(at)
            kept = lax.dynamic_index_in_dim(data, bit, at_now, keepdims=False)
            out = lax.dynamic_index_in_dim(data, 1 - bit, at_now, keepdims=False)
            data = add_bf16(kept, exchange(out, axis, 1 << b))
        pieces.append(data)
    data = jnp.concatenate(pieces, axis=1)
    for b in range(1, dp_bits):
        recv = exchange(data, "dp", 1 << b)
        first_half = (dp_i >> b) % 2 == 0
        data = jnp.where(first_half, jnp.concatenate([data, recv], 0), jnp.concatenate([recv, data], 0))
    pieces = [data]
    part = jnp.concatenate(pieces, axis=1)
    back = exchange(part, "dp", 1)
    mine = [part[:, :width], part[:, width:]]
    other = [back[:, :width], back[:, width:]]
    return (
        pick(mine[0], other[0]).astype(jnp.float32),
        pick(mine[1], other[1]).astype(jnp.float32),
        pick(other[0], mine[0]).astype(jnp.float32),
        pick(other[1], mine[1]).astype(jnp.float32),
    )


def body(layer_input, w_query, w_key, w_value, w_out, offsets, grad_out):
    rows = layer_input[0]
    cot = grad_out[0]
    tok = rows.shape[0]
    width = rows.shape[1]
    head = width // HEADS
    levels = lax.axis_size("seq").bit_length() - 1
    query = jnp.dot(rows, w_query, preferred_element_type=jnp.float32).astype(jnp.bfloat16)
    keys_local = jnp.dot(rows, w_key, preferred_element_type=jnp.float32).astype(jnp.bfloat16)
    values_local = jnp.dot(rows, w_value, preferred_element_type=jnp.float32).astype(jnp.bfloat16)
    remote = swap_blocks(keys_local, values_local, offsets, levels)
    d_att = jnp.dot(cot, w_out.T, preferred_element_type=jnp.float32).astype(jnp.bfloat16)
    attended, dquery, dkey_sum, dvalue_sum, back = attention(query, keys_local, values_local, d_att, remote, head)
    result = jnp.dot(attended, w_out, preferred_element_type=jnp.float32).astype(jnp.bfloat16)
    for level in range(levels):
        returned = partner(back[level], "seq", level).astype(jnp.float32)
        start = offsets[level] * BLOCK
        dkey_sum = lax.dynamic_update_slice_in_dim(
            dkey_sum, lax.dynamic_slice_in_dim(dkey_sum, start, BLOCK, 0) + returned[0], start, 0
        )
        dvalue_sum = lax.dynamic_update_slice_in_dim(
            dvalue_sum,
            lax.dynamic_slice_in_dim(dvalue_sum, start, BLOCK, 0) + returned[1],
            start,
            0,
        )
    dkey = dkey_sum.astype(jnp.bfloat16)
    dvalue = dvalue_sum.astype(jnp.bfloat16)
    total = jnp.dot(dquery, w_query.T, preferred_element_type=jnp.float32)
    total = total + jnp.dot(dkey, w_key.T, preferred_element_type=jnp.float32)
    total = total + jnp.dot(dvalue, w_value.T, preferred_element_type=jnp.float32)
    grad_input = total.astype(jnp.bfloat16)
    sources = ((rows, dquery), (rows, dkey), (rows, dvalue), (attended, cot))
    grads = reduce_gradients(sources)
    return (result[None], grad_input[None]) + grads


def solution(mesh):
    return jax.shard_map(
        body,
        mesh=mesh,
        in_specs=(P("dp", "seq", None), P(), P(), P(), P(), P(), P("dp", "seq", None)),
        out_specs=(
            P("dp", "seq", None),
            P("dp", "seq", None),
            P("seq", None),
            P("seq", None),
            P("seq", None),
            P("seq", None),
        ),
        check_vma=False,
    )
```

```python
import functools

import jax
import jax.numpy as jnp
from jax import lax
from jax.experimental import pallas as pl
from jax.experimental.pallas import tpu as pltpu
from jax.sharding import PartitionSpec as P

HEADS = 16
BLOCK = 128
LANES = 128


def partner(array, axis, apart):
    return lax.ppermute(array, axis, [(i, i ^ 1 << apart) for i in range(lax.axis_size(axis))])


def swap_blocks(keys_local, values_local, offsets, levels, lo, hi):
    remote = []
    for level in range(levels):
        start = offsets[level] * BLOCK
        pair = jnp.stack(
            [
                lax.dynamic_slice_in_dim(keys_local[:, lo:hi], start, BLOCK, 0),
                lax.dynamic_slice_in_dim(values_local[:, lo:hi], start, BLOCK, 0),
            ]
        )
        remote.append(partner(pair, "seq", level))
    return remote


def attention_kernel(q_ref, k_ref, v_ref, do_ref, *refs, head, scale):
    remote = refs[:-5]
    att_ref, dq_ref, dk_ref, dv_ref, back_ref = refs[-5:]
    q = q_ref[...]
    k = jnp.concatenate([k_ref[...]] + [r[0] for r in remote], axis=0)
    v = jnp.concatenate([v_ref[...]] + [r[1] for r in remote], axis=0)
    do = do_ref[...]
    width = q.shape[1]
    lane = lax.broadcasted_iota(jnp.int32, (1, width), 1)
    row = lax.broadcasted_iota(jnp.int32, (width, 1), 0)
    q_t = q.T
    do_t = do.T
    probs, grads, v_parts, k_parts, q_parts, do_parts = [], [], [], [], [], []
    for j in range(width // head):
        inside = (lane >= j * head) & (lane < (j + 1) * head)
        rows_in = (row >= j * head) & (row < (j + 1) * head)
        qm = jnp.where(inside, q * jnp.asarray(scale, q.dtype), jnp.zeros_like(q))
        dom = jnp.where(inside, do, jnp.zeros_like(do))
        s = lax.dot_general(qm, k, (((1,), (1,)), ((), ())), preferred_element_type=jnp.float32)
        top = jnp.max(s, axis=-1, keepdims=True)
        e = jnp.exp(s - top)
        p = e * (1.0 / jnp.sum(e, axis=-1, keepdims=True))
        dp = lax.dot_general(dom, v, (((1,), (1,)), ((), ())), preferred_element_type=jnp.float32)
        delta = jnp.sum(p * dp, axis=-1, keepdims=True)
        probs.append(p.astype(jnp.bfloat16))
        grads.append((p * (dp - delta) * scale).astype(jnp.bfloat16))
        v_parts.append(jnp.where(inside, v, jnp.zeros_like(v)))
        k_parts.append(jnp.where(inside, k, jnp.zeros_like(k)))
        q_parts.append(jnp.where(rows_in, q_t, jnp.zeros_like(q_t)))
        do_parts.append(jnp.where(rows_in, do_t, jnp.zeros_like(do_t)))
    att = jnp.dot(jnp.concatenate(probs, 1), jnp.concatenate(v_parts, 0), preferred_element_type=jnp.float32)
    dq = jnp.dot(jnp.concatenate(grads, 1), jnp.concatenate(k_parts, 0), preferred_element_type=jnp.float32)
    dk_t = jnp.dot(jnp.concatenate(q_parts, 1), jnp.concatenate(grads, 0), preferred_element_type=jnp.float32)
    dv_t = jnp.dot(jnp.concatenate(do_parts, 1), jnp.concatenate(probs, 0), preferred_element_type=jnp.float32)
    att_ref[...] = att.astype(att_ref.dtype)
    dq_ref[...] = dq.astype(dq_ref.dtype)
    dk = dk_t.T
    dv = dv_t.T
    tok = q.shape[0]
    dk_ref[...] = dk[:tok]
    dv_ref[...] = dv[:tok]
    low = tok
    for level, r in enumerate(remote):
        high = low + r.shape[1]
        back_ref[level, 0] = dk[low:high].astype(back_ref.dtype)
        back_ref[level, 1] = dv[low:high].astype(back_ref.dtype)
        low = high


def attention(query, keys, values, d_att, remote, head, lo, hi):
    tok = query.shape[0]
    width = hi - lo
    levels = len(remote)
    block = remote[0].shape[1]
    total = tok + levels * block
    steps = width // LANES
    base = lo // LANES
    fspec = pl.BlockSpec((tok, LANES), lambda i: (0, i + base))
    qspec = pl.BlockSpec((tok, LANES), lambda i: (0, i))
    rspec = pl.BlockSpec((2, block, LANES), lambda i: (0, 0, i))
    bspec = pl.BlockSpec((levels, 2, block, LANES), lambda i: (0, 0, 0, i))
    return pl.pallas_call(
        functools.partial(attention_kernel, head=head, scale=head ** -0.5),
        grid=(steps,),
        in_specs=[fspec] * 4 + [rspec] * levels,
        out_specs=[qspec] * 4 + [bspec],
        out_shape=[
            jax.ShapeDtypeStruct((tok, width), jnp.bfloat16),
            jax.ShapeDtypeStruct((tok, width), jnp.bfloat16),
            jax.ShapeDtypeStruct((tok, width), jnp.float32),
            jax.ShapeDtypeStruct((tok, width), jnp.float32),
            jax.ShapeDtypeStruct((levels, 2, block, width), jnp.bfloat16),
        ],
        compiler_params=pltpu.CompilerParams(vmem_limit_bytes=60 * 1024 * 1024),
        cost_estimate=pl.CostEstimate(
            flops=12 * tok * total * width * (LANES // head),
            transcendentals=tok * total * (width // head),
            bytes_accessed=4 * tok * width + 12 * total * width,
        ),
    )(query, keys, values, d_att, *remote)


def exchange(array, axis, mask):
    return lax.ppermute(array, axis, [(i, i ^ mask) for i in range(lax.axis_size(axis))])


def add_bf16(a, b):
    return (a.astype(jnp.float32) + b.astype(jnp.float32)).astype(jnp.bfloat16)


def term(left, right, lo, hi):
    return jnp.dot(left.T, right[:, lo:hi], preferred_element_type=jnp.float32).astype(jnp.bfloat16)


def reduce_gradients(sources):
    n_dp = lax.axis_size("dp")
    n_seq = lax.axis_size("seq")
    seq_bits = n_seq.bit_length() - 1
    dp_bits = n_dp.bit_length() - 1
    width = sources[0][1].shape[1]
    rows = sources[0][0].shape[1]
    blk = rows // n_seq
    dp_i = lax.axis_index("dp")
    seq_i = lax.axis_index("seq")
    low = dp_i % 2 == 0

    def pick(a, b):
        return jnp.where(low, a, b)

    keep = [
        (sources[0][0], pick(sources[0][1], sources[2][1])),
        (pick(sources[1][0], sources[3][0]), pick(sources[1][1], sources[3][1])),
    ]
    send = [
        (sources[2][0], pick(sources[2][1], sources[0][1])),
        (pick(sources[3][0], sources[1][0]), pick(sources[3][1], sources[1][1])),
    ]
    seq_dims = [("seq", b) for b in range(seq_bits)]
    dp_dims = [("dp", b) for b in range(1, dp_bits)]
    if seq_bits >= 2:
        orders = [
            seq_dims[:2] + dp_dims + seq_dims[2:],
            seq_dims[1::-1] + seq_dims[2:] + dp_dims,
        ]
    else:
        orders = [seq_dims + dp_dims] * 2
    shape = [2] * seq_bits + [2] * (dp_bits - 1) + [blk >> (dp_bits - 1)]
    sends = [term(*send[g], 0, width) for g in range(2)]
    keeps = [term(*keep[g], 0, width) for g in range(2)]
    got = exchange(sends, "dp", 1)
    pieces = []
    for g in range(2):
        data = add_bf16(keeps[g], got[g]).reshape(shape + [width])
        removed = []
        for axis, b in orders[g]:
            if axis == "seq":
                at = seq_bits - 1 - b
                bit = (seq_i >> b) % 2
            else:
                at = seq_bits + (dp_bits - 1 - b)
                bit = (dp_i >> b) % 2
            at_now = at - sum(1 for r in removed if r < at)
            removed.append(at)
            kept = lax.dynamic_index_in_dim(data, bit, at_now, keepdims=False)
            out = lax.dynamic_index_in_dim(data, 1 - bit, at_now, keepdims=False)
            data = add_bf16(kept, exchange(out, axis, 1 << b))
        pieces.append(data)
    data = jnp.concatenate(pieces, axis=1)
    for b in range(1, dp_bits):
        recv = exchange(data, "dp", 1 << b)
        first_half = (dp_i >> b) % 2 == 0
        data = jnp.where(first_half, jnp.concatenate([data, recv], 0), jnp.concatenate([recv, data], 0))
    pieces = [data]
    part = jnp.concatenate(pieces, axis=1)
    back = exchange(part, "dp", 1)
    mine = [part[:, :width], part[:, width:]]
    other = [back[:, :width], back[:, width:]]
    return (
        pick(mine[0], other[0]).astype(jnp.float32),
        pick(mine[1], other[1]).astype(jnp.float32),
        pick(other[0], mine[0]).astype(jnp.float32),
        pick(other[1], mine[1]).astype(jnp.float32),
    )


def body(layer_input, w_query, w_key, w_value, w_out, offsets, grad_out):
    rows = layer_input[0]
    cot = grad_out[0]
    tok = rows.shape[0]
    width = rows.shape[1]
    head = width // HEADS
    levels = lax.axis_size("seq").bit_length() - 1
    query = jnp.dot(rows, w_query, preferred_element_type=jnp.float32).astype(jnp.bfloat16)
    keys_local = jnp.dot(rows, w_key, preferred_element_type=jnp.float32).astype(jnp.bfloat16)
    values_local = jnp.dot(rows, w_value, preferred_element_type=jnp.float32).astype(jnp.bfloat16)
    half = (width // LANES) // 2 * LANES
    spans = [(0, half), (half, width)]
    remotes = [swap_blocks(keys_local, values_local, offsets, levels, lo, hi) for lo, hi in spans]
    d_att = jnp.dot(cot, w_out.T, preferred_element_type=jnp.float32).astype(jnp.bfloat16)
    outs = [
        attention(query, keys_local, values_local, d_att, remote, head, lo, hi)
        for remote, (lo, hi) in zip(remotes, spans)
    ]
    attended = jnp.concatenate([o[0] for o in outs], axis=1)
    dquery = jnp.concatenate([o[1] for o in outs], axis=1)
    result = jnp.dot(attended, w_out, preferred_element_type=jnp.float32).astype(jnp.bfloat16)
    dkeys = []
    dvalues = []
    for _, _, dkey_sum, dvalue_sum, back in outs:
        for level in range(levels):
            returned = partner(back[level], "seq", level).astype(jnp.float32)
            start = offsets[level] * BLOCK
            dkey_sum = lax.dynamic_update_slice_in_dim(
                dkey_sum, lax.dynamic_slice_in_dim(dkey_sum, start, BLOCK, 0) + returned[0], start, 0
            )
            dvalue_sum = lax.dynamic_update_slice_in_dim(
                dvalue_sum,
                lax.dynamic_slice_in_dim(dvalue_sum, start, BLOCK, 0) + returned[1],
                start,
                0,
            )
        dkeys.append(dkey_sum.astype(jnp.bfloat16))
        dvalues.append(dvalue_sum.astype(jnp.bfloat16))
    dkey = jnp.concatenate(dkeys, axis=1)
    dvalue = jnp.concatenate(dvalues, axis=1)
    total = jnp.dot(dquery, w_query.T, preferred_element_type=jnp.float32)
    total = total + jnp.dot(dkey, w_key.T, preferred_element_type=jnp.float32)
    total = total + jnp.dot(dvalue, w_value.T, preferred_element_type=jnp.float32)
    grad_input = total.astype(jnp.bfloat16)
    sources = ((rows, dquery), (rows, dkey), (rows, dvalue), (attended, cot))
    grads = reduce_gradients(sources)
    return (result[None], grad_input[None]) + grads


def solution(mesh):
    return jax.shard_map(
        body,
        mesh=mesh,
        in_specs=(P("dp", "seq", None), P(), P(), P(), P(), P(), P("dp", "seq", None)),
        out_specs=(
            P("dp", "seq", None),
            P("dp", "seq", None),
            P("seq", None),
            P("seq", None),
            P("seq", None),
            P("seq", None),
        ),
        check_vma=False,
    )
```

```python
import functools

import jax
import jax.numpy as jnp
from jax import lax
from jax.experimental import pallas as pl
from jax.experimental.pallas import tpu as pltpu
from jax.sharding import PartitionSpec as P

HEADS = 16
BLOCK = 128
LANES = 128
SPLIT = 4


def partner(array, axis, apart):
    return lax.ppermute(array, axis, [(i, i ^ 1 << apart) for i in range(lax.axis_size(axis))])


def swap_blocks(keys_local, values_local, offsets, levels, lo, hi):
    remote = []
    for level in range(levels):
        start = offsets[level] * BLOCK
        pair = jnp.stack(
            [
                lax.dynamic_slice_in_dim(keys_local[:, lo:hi], start, BLOCK, 0),
                lax.dynamic_slice_in_dim(values_local[:, lo:hi], start, BLOCK, 0),
            ]
        )
        remote.append(partner(pair, "seq", level))
    return remote


def attention_kernel(q_ref, k_ref, v_ref, do_ref, *refs, head, scale):
    remote = refs[:-5]
    att_ref, dq_ref, dk_ref, dv_ref, back_ref = refs[-5:]
    q = q_ref[...]
    k = jnp.concatenate([k_ref[...]] + [r[0] for r in remote], axis=0)
    v = jnp.concatenate([v_ref[...]] + [r[1] for r in remote], axis=0)
    do = do_ref[...]
    width = q.shape[1]
    lane = lax.broadcasted_iota(jnp.int32, (1, width), 1)
    row = lax.broadcasted_iota(jnp.int32, (width, 1), 0)
    q_t = q.T
    do_t = do.T
    probs, grads, v_parts, k_parts, q_parts, do_parts = [], [], [], [], [], []
    for j in range(width // head):
        inside = (lane >= j * head) & (lane < (j + 1) * head)
        rows_in = (row >= j * head) & (row < (j + 1) * head)
        qm = jnp.where(inside, q * jnp.asarray(scale, q.dtype), jnp.zeros_like(q))
        dom = jnp.where(inside, do, jnp.zeros_like(do))
        s = lax.dot_general(qm, k, (((1,), (1,)), ((), ())), preferred_element_type=jnp.float32)
        top = jnp.max(s, axis=-1, keepdims=True)
        e = jnp.exp(s - top)
        p = e * (1.0 / jnp.sum(e, axis=-1, keepdims=True))
        dp = lax.dot_general(dom, v, (((1,), (1,)), ((), ())), preferred_element_type=jnp.float32)
        delta = jnp.sum(p * dp, axis=-1, keepdims=True)
        probs.append(p.astype(jnp.bfloat16))
        grads.append((p * (dp - delta) * scale).astype(jnp.bfloat16))
        v_parts.append(jnp.where(inside, v, jnp.zeros_like(v)))
        k_parts.append(jnp.where(inside, k, jnp.zeros_like(k)))
        q_parts.append(jnp.where(rows_in, q_t, jnp.zeros_like(q_t)))
        do_parts.append(jnp.where(rows_in, do_t, jnp.zeros_like(do_t)))
    att = jnp.dot(jnp.concatenate(probs, 1), jnp.concatenate(v_parts, 0), preferred_element_type=jnp.float32)
    dq = jnp.dot(jnp.concatenate(grads, 1), jnp.concatenate(k_parts, 0), preferred_element_type=jnp.float32)
    dk_t = jnp.dot(jnp.concatenate(q_parts, 1), jnp.concatenate(grads, 0), preferred_element_type=jnp.float32)
    dv_t = jnp.dot(jnp.concatenate(do_parts, 1), jnp.concatenate(probs, 0), preferred_element_type=jnp.float32)
    att_ref[...] = att.astype(att_ref.dtype)
    dq_ref[...] = dq.astype(dq_ref.dtype)
    dk = dk_t.T
    dv = dv_t.T
    tok = q.shape[0]
    dk_ref[...] = dk[:tok]
    dv_ref[...] = dv[:tok]
    low = tok
    for level, r in enumerate(remote):
        high = low + r.shape[1]
        back_ref[level, 0] = dk[low:high].astype(back_ref.dtype)
        back_ref[level, 1] = dv[low:high].astype(back_ref.dtype)
        low = high


def attention(query, keys, values, d_att, remote, head, lo, hi):
    tok = query.shape[0]
    width = hi - lo
    levels = len(remote)
    block = remote[0].shape[1]
    total = tok + levels * block
    steps = width // LANES
    base = lo // LANES
    fspec = pl.BlockSpec((tok, LANES), lambda i: (0, i + base))
    qspec = pl.BlockSpec((tok, LANES), lambda i: (0, i))
    rspec = pl.BlockSpec((2, block, LANES), lambda i: (0, 0, i))
    bspec = pl.BlockSpec((levels, 2, block, LANES), lambda i: (0, 0, 0, i))
    return pl.pallas_call(
        functools.partial(attention_kernel, head=head, scale=head ** -0.5),
        grid=(steps,),
        in_specs=[fspec] * 4 + [rspec] * levels,
        out_specs=[qspec] * 4 + [bspec],
        out_shape=[
            jax.ShapeDtypeStruct((tok, width), jnp.bfloat16),
            jax.ShapeDtypeStruct((tok, width), jnp.bfloat16),
            jax.ShapeDtypeStruct((tok, width), jnp.float32),
            jax.ShapeDtypeStruct((tok, width), jnp.float32),
            jax.ShapeDtypeStruct((levels, 2, block, width), jnp.bfloat16),
        ],
        compiler_params=pltpu.CompilerParams(vmem_limit_bytes=60 * 1024 * 1024),
        cost_estimate=pl.CostEstimate(
            flops=12 * tok * total * width * (LANES // head),
            transcendentals=tok * total * (width // head),
            bytes_accessed=4 * tok * width + 12 * total * width,
        ),
    )(query, keys, values, d_att, *remote)


def exchange(array, axis, mask):
    return lax.ppermute(array, axis, [(i, i ^ mask) for i in range(lax.axis_size(axis))])


def add_bf16(a, b):
    return (a.astype(jnp.float32) + b.astype(jnp.float32)).astype(jnp.bfloat16)


def term(left, right, lo, hi):
    return jnp.dot(left.T, right[:, lo:hi], preferred_element_type=jnp.float32).astype(jnp.bfloat16)


def reduce_gradients(sources):
    n_dp = lax.axis_size("dp")
    n_seq = lax.axis_size("seq")
    seq_bits = n_seq.bit_length() - 1
    dp_bits = n_dp.bit_length() - 1
    width = sources[0][1].shape[1]
    rows = sources[0][0].shape[1]
    blk = rows // n_seq
    dp_i = lax.axis_index("dp")
    seq_i = lax.axis_index("seq")
    low = dp_i % 2 == 0

    def pick(a, b):
        return jnp.where(low, a, b)

    keep = [
        (sources[0][0], pick(sources[0][1], sources[2][1])),
        (pick(sources[1][0], sources[3][0]), pick(sources[1][1], sources[3][1])),
    ]
    send = [
        (sources[2][0], pick(sources[2][1], sources[0][1])),
        (pick(sources[3][0], sources[1][0]), pick(sources[3][1], sources[1][1])),
    ]
    seq_dims = [("seq", b) for b in range(seq_bits)]
    dp_dims = [("dp", b) for b in range(1, dp_bits)]
    if seq_bits >= 2:
        orders = [
            seq_dims[:2] + dp_dims + seq_dims[2:],
            seq_dims[1::-1] + seq_dims[2:] + dp_dims,
        ]
    else:
        orders = [seq_dims + dp_dims] * 2
    shape = [2] * seq_bits + [2] * (dp_bits - 1) + [blk >> (dp_bits - 1)]
    sends = [term(*send[g], 0, width) for g in range(2)]
    keeps = [term(*keep[g], 0, width) for g in range(2)]
    got = exchange(sends, "dp", 1)
    pieces = []
    for g in range(2):
        data = add_bf16(keeps[g], got[g]).reshape(shape + [width])
        removed = []
        for axis, b in orders[g]:
            if axis == "seq":
                at = seq_bits - 1 - b
                bit = (seq_i >> b) % 2
            else:
                at = seq_bits + (dp_bits - 1 - b)
                bit = (dp_i >> b) % 2
            at_now = at - sum(1 for r in removed if r < at)
            removed.append(at)
            kept = lax.dynamic_index_in_dim(data, bit, at_now, keepdims=False)
            out = lax.dynamic_index_in_dim(data, 1 - bit, at_now, keepdims=False)
            data = add_bf16(kept, exchange(out, axis, 1 << b))
        pieces.append(data)
    data = jnp.concatenate(pieces, axis=1)
    for b in range(1, dp_bits):
        recv = exchange(data, "dp", 1 << b)
        first_half = (dp_i >> b) % 2 == 0
        data = jnp.where(first_half, jnp.concatenate([data, recv], 0), jnp.concatenate([recv, data], 0))
    pieces = [data]
    part = jnp.concatenate(pieces, axis=1)
    back = exchange(part, "dp", 1)
    mine = [part[:, :width], part[:, width:]]
    other = [back[:, :width], back[:, width:]]
    return (
        pick(mine[0], other[0]).astype(jnp.float32),
        pick(mine[1], other[1]).astype(jnp.float32),
        pick(other[0], mine[0]).astype(jnp.float32),
        pick(other[1], mine[1]).astype(jnp.float32),
    )


def body(layer_input, w_query, w_key, w_value, w_out, offsets, grad_out):
    rows = layer_input[0]
    cot = grad_out[0]
    tok = rows.shape[0]
    width = rows.shape[1]
    head = width // HEADS
    levels = lax.axis_size("seq").bit_length() - 1
    query = jnp.dot(rows, w_query, preferred_element_type=jnp.float32).astype(jnp.bfloat16)
    keys_local = jnp.dot(rows, w_key, preferred_element_type=jnp.float32).astype(jnp.bfloat16)
    values_local = jnp.dot(rows, w_value, preferred_element_type=jnp.float32).astype(jnp.bfloat16)
    units = width // LANES
    cuts = [units * c // SPLIT * LANES for c in range(SPLIT + 1)]
    spans = list(zip(cuts[:-1], cuts[1:]))
    remotes = [swap_blocks(keys_local, values_local, offsets, levels, lo, hi) for lo, hi in spans]
    d_att = jnp.dot(cot, w_out.T, preferred_element_type=jnp.float32).astype(jnp.bfloat16)
    outs = [
        attention(query, keys_local, values_local, d_att, remote, head, lo, hi)
        for remote, (lo, hi) in zip(remotes, spans)
    ]
    attended = jnp.concatenate([o[0] for o in outs], axis=1)
    dquery = jnp.concatenate([o[1] for o in outs], axis=1)
    result = jnp.dot(attended, w_out, preferred_element_type=jnp.float32).astype(jnp.bfloat16)
    dkeys = []
    dvalues = []
    for _, _, dkey_sum, dvalue_sum, back in outs:
        for level in range(levels):
            returned = partner(back[level], "seq", level).astype(jnp.float32)
            start = offsets[level] * BLOCK
            dkey_sum = lax.dynamic_update_slice_in_dim(
                dkey_sum, lax.dynamic_slice_in_dim(dkey_sum, start, BLOCK, 0) + returned[0], start, 0
            )
            dvalue_sum = lax.dynamic_update_slice_in_dim(
                dvalue_sum,
                lax.dynamic_slice_in_dim(dvalue_sum, start, BLOCK, 0) + returned[1],
                start,
                0,
            )
        dkeys.append(dkey_sum.astype(jnp.bfloat16))
        dvalues.append(dvalue_sum.astype(jnp.bfloat16))
    dkey = jnp.concatenate(dkeys, axis=1)
    dvalue = jnp.concatenate(dvalues, axis=1)
    total = jnp.dot(dquery, w_query.T, preferred_element_type=jnp.float32)
    total = total + jnp.dot(dkey, w_key.T, preferred_element_type=jnp.float32)
    total = total + jnp.dot(dvalue, w_value.T, preferred_element_type=jnp.float32)
    grad_input = total.astype(jnp.bfloat16)
    sources = ((rows, dquery), (rows, dkey), (rows, dvalue), (attended, cot))
    grads = reduce_gradients(sources)
    return (result[None], grad_input[None]) + grads


def solution(mesh):
    return jax.shard_map(
        body,
        mesh=mesh,
        in_specs=(P("dp", "seq", None), P(), P(), P(), P(), P(), P("dp", "seq", None)),
        out_specs=(
            P("dp", "seq", None),
            P("dp", "seq", None),
            P("seq", None),
            P("seq", None),
            P("seq", None),
            P("seq", None),
        ),
        check_vma=False,
    )
```

```python
import functools

import jax
import jax.numpy as jnp
from jax import lax
from jax.experimental import pallas as pl
from jax.experimental.pallas import tpu as pltpu
from jax.sharding import PartitionSpec as P

HEADS = 16
BLOCK = 128
LANES = 128


def partner(array, axis, apart):
    return lax.ppermute(array, axis, [(i, i ^ 1 << apart) for i in range(lax.axis_size(axis))])


def swap_blocks(keys_local, values_local, offsets, levels, lo, hi):
    remote = []
    for level in range(levels):
        start = offsets[level] * BLOCK
        pair = jnp.stack(
            [
                lax.dynamic_slice_in_dim(keys_local[:, lo:hi], start, BLOCK, 0),
                lax.dynamic_slice_in_dim(values_local[:, lo:hi], start, BLOCK, 0),
            ]
        )
        remote.append(partner(pair, "seq", level))
    return remote


def attention_kernel(q_ref, k_ref, v_ref, do_ref, *refs, head, scale):
    remote = refs[:-5]
    att_ref, dq_ref, dk_ref, dv_ref, back_ref = refs[-5:]
    q = q_ref[...]
    k = jnp.concatenate([k_ref[...]] + [r[0] for r in remote], axis=0)
    v = jnp.concatenate([v_ref[...]] + [r[1] for r in remote], axis=0)
    do = do_ref[...]
    width = q.shape[1]
    lane = lax.broadcasted_iota(jnp.int32, (1, width), 1)
    row = lax.broadcasted_iota(jnp.int32, (width, 1), 0)
    q_t = q.T
    do_t = do.T
    probs, grads, v_parts, k_parts, q_parts, do_parts = [], [], [], [], [], []
    for j in range(width // head):
        inside = (lane >= j * head) & (lane < (j + 1) * head)
        rows_in = (row >= j * head) & (row < (j + 1) * head)
        qm = jnp.where(inside, q * jnp.asarray(scale, q.dtype), jnp.zeros_like(q))
        dom = jnp.where(inside, do, jnp.zeros_like(do))
        s = lax.dot_general(qm, k, (((1,), (1,)), ((), ())), preferred_element_type=jnp.float32)
        top = jnp.max(s, axis=-1, keepdims=True)
        e = jnp.exp(s - top)
        p = e * (1.0 / jnp.sum(e, axis=-1, keepdims=True))
        dp = lax.dot_general(dom, v, (((1,), (1,)), ((), ())), preferred_element_type=jnp.float32)
        delta = jnp.sum(p * dp, axis=-1, keepdims=True)
        probs.append(p.astype(jnp.bfloat16))
        grads.append((p * (dp - delta) * scale).astype(jnp.bfloat16))
        v_parts.append(jnp.where(inside, v, jnp.zeros_like(v)))
        k_parts.append(jnp.where(inside, k, jnp.zeros_like(k)))
        q_parts.append(jnp.where(rows_in, q_t, jnp.zeros_like(q_t)))
        do_parts.append(jnp.where(rows_in, do_t, jnp.zeros_like(do_t)))
    att = jnp.dot(jnp.concatenate(probs, 1), jnp.concatenate(v_parts, 0), preferred_element_type=jnp.float32)
    dq = jnp.dot(jnp.concatenate(grads, 1), jnp.concatenate(k_parts, 0), preferred_element_type=jnp.float32)
    dk_t = jnp.dot(jnp.concatenate(q_parts, 1), jnp.concatenate(grads, 0), preferred_element_type=jnp.float32)
    dv_t = jnp.dot(jnp.concatenate(do_parts, 1), jnp.concatenate(probs, 0), preferred_element_type=jnp.float32)
    att_ref[...] = att.astype(att_ref.dtype)
    dq_ref[...] = dq.astype(dq_ref.dtype)
    dk = dk_t.T
    dv = dv_t.T
    tok = q.shape[0]
    dk_ref[...] = dk[:tok]
    dv_ref[...] = dv[:tok]
    low = tok
    for level, r in enumerate(remote):
        high = low + r.shape[1]
        back_ref[level, 0] = dk[low:high].astype(back_ref.dtype)
        back_ref[level, 1] = dv[low:high].astype(back_ref.dtype)
        low = high


def attention(query, keys, values, d_att, remote, head, lo, hi):
    tok = query.shape[0]
    width = hi - lo
    levels = len(remote)
    block = remote[0].shape[1]
    total = tok + levels * block
    steps = width // LANES
    base = lo // LANES
    fspec = pl.BlockSpec((tok, LANES), lambda i: (0, i + base))
    qspec = pl.BlockSpec((tok, LANES), lambda i: (0, i))
    rspec = pl.BlockSpec((2, block, LANES), lambda i: (0, 0, i))
    bspec = pl.BlockSpec((levels, 2, block, LANES), lambda i: (0, 0, 0, i))
    return pl.pallas_call(
        functools.partial(attention_kernel, head=head, scale=head ** -0.5),
        grid=(steps,),
        in_specs=[fspec] * 4 + [rspec] * levels,
        out_specs=[qspec] * 4 + [bspec],
        out_shape=[
            jax.ShapeDtypeStruct((tok, width), jnp.bfloat16),
            jax.ShapeDtypeStruct((tok, width), jnp.bfloat16),
            jax.ShapeDtypeStruct((tok, width), jnp.float32),
            jax.ShapeDtypeStruct((tok, width), jnp.float32),
            jax.ShapeDtypeStruct((levels, 2, block, width), jnp.bfloat16),
        ],
        compiler_params=pltpu.CompilerParams(vmem_limit_bytes=60 * 1024 * 1024),
        cost_estimate=pl.CostEstimate(
            flops=12 * tok * total * width * (LANES // head),
            transcendentals=tok * total * (width // head),
            bytes_accessed=4 * tok * width + 12 * total * width,
        ),
    )(query, keys, values, d_att, *remote)


def exchange(array, axis, mask):
    return lax.ppermute(array, axis, [(i, i ^ mask) for i in range(lax.axis_size(axis))])


def add_bf16(a, b):
    return (a.astype(jnp.float32) + b.astype(jnp.float32)).astype(jnp.bfloat16)


def term(left, right, lo, hi):
    return jnp.dot(left.T, right[:, lo:hi], preferred_element_type=jnp.float32).astype(jnp.bfloat16)


def reduce_gradients(sources):
    n_dp = lax.axis_size("dp")
    n_seq = lax.axis_size("seq")
    seq_bits = n_seq.bit_length() - 1
    dp_bits = n_dp.bit_length() - 1
    width = sources[0][1].shape[1]
    rows = sources[0][0].shape[1]
    blk = rows // n_seq
    dp_i = lax.axis_index("dp")
    seq_i = lax.axis_index("seq")
    low = dp_i % 2 == 0

    def pick(a, b):
        return jnp.where(low, a, b)

    keep = [
        (sources[0][0], pick(sources[0][1], sources[2][1])),
        (pick(sources[1][0], sources[3][0]), pick(sources[1][1], sources[3][1])),
    ]
    send = [
        (sources[2][0], pick(sources[2][1], sources[0][1])),
        (pick(sources[3][0], sources[1][0]), pick(sources[3][1], sources[1][1])),
    ]
    seq_dims = [("seq", b) for b in range(seq_bits)]
    dp_dims = [("dp", b) for b in range(1, dp_bits)]
    if seq_bits >= 2:
        orders = [
            seq_dims[:2] + dp_dims + seq_dims[2:],
            seq_dims[1::-1] + seq_dims[2:] + dp_dims,
        ]
    else:
        orders = [seq_dims + dp_dims] * 2
    shape = [2] * seq_bits + [2] * (dp_bits - 1) + [blk >> (dp_bits - 1)]
    sends = [term(*send[g], 0, width) for g in range(2)]
    keeps = [term(*keep[g], 0, width) for g in range(2)]
    got = exchange(sends, "dp", 1)
    pieces = []
    for g in range(2):
        data = add_bf16(keeps[g], got[g]).reshape(shape + [width])
        removed = []
        for axis, b in orders[g]:
            if axis == "seq":
                at = seq_bits - 1 - b
                bit = (seq_i >> b) % 2
            else:
                at = seq_bits + (dp_bits - 1 - b)
                bit = (dp_i >> b) % 2
            at_now = at - sum(1 for r in removed if r < at)
            removed.append(at)
            kept = lax.dynamic_index_in_dim(data, bit, at_now, keepdims=False)
            out = lax.dynamic_index_in_dim(data, 1 - bit, at_now, keepdims=False)
            data = add_bf16(kept, exchange(out, axis, 1 << b))
        pieces.append(data)
    data = jnp.concatenate(pieces, axis=1)
    for b in range(1, dp_bits):
        recv = exchange(data, "dp", 1 << b)
        first_half = (dp_i >> b) % 2 == 0
        data = jnp.where(first_half, jnp.concatenate([data, recv], 0), jnp.concatenate([recv, data], 0))
    pieces = [data]
    part = jnp.concatenate(pieces, axis=1)
    back = exchange(part, "dp", 1)
    mine = [part[:, :width], part[:, width:]]
    other = [back[:, :width], back[:, width:]]
    return (
        pick(mine[0], other[0]).astype(jnp.float32),
        pick(mine[1], other[1]).astype(jnp.float32),
        pick(other[0], mine[0]).astype(jnp.float32),
        pick(other[1], mine[1]).astype(jnp.float32),
    )


def body(layer_input, w_query, w_key, w_value, w_out, offsets, grad_out):
    rows = layer_input[0]
    cot = grad_out[0]
    tok = rows.shape[0]
    width = rows.shape[1]
    head = width // HEADS
    levels = lax.axis_size("seq").bit_length() - 1
    query = jnp.dot(rows, w_query, preferred_element_type=jnp.float32).astype(jnp.bfloat16)
    keys_local = jnp.dot(rows, w_key, preferred_element_type=jnp.float32).astype(jnp.bfloat16)
    values_local = jnp.dot(rows, w_value, preferred_element_type=jnp.float32).astype(jnp.bfloat16)
    half = (width // LANES) // 2 * LANES
    spans = [(0, half), (half, width)]
    remotes = [swap_blocks(keys_local, values_local, offsets, levels, *spans[0])]
    later_keys, later_values, _ = lax.optimization_barrier((keys_local, values_local, remotes[0]))
    remotes.append(swap_blocks(later_keys, later_values, offsets, levels, *spans[1]))
    d_att = jnp.dot(cot, w_out.T, preferred_element_type=jnp.float32).astype(jnp.bfloat16)
    outs = [
        attention(query, keys_local, values_local, d_att, remote, head, lo, hi)
        for remote, (lo, hi) in zip(remotes, spans)
    ]
    attended = jnp.concatenate([o[0] for o in outs], axis=1)
    dquery = jnp.concatenate([o[1] for o in outs], axis=1)
    result = jnp.dot(attended, w_out, preferred_element_type=jnp.float32).astype(jnp.bfloat16)
    dkeys = []
    dvalues = []
    for _, _, dkey_sum, dvalue_sum, back in outs:
        for level in range(levels):
            returned = partner(back[level], "seq", level).astype(jnp.float32)
            start = offsets[level] * BLOCK
            dkey_sum = lax.dynamic_update_slice_in_dim(
                dkey_sum, lax.dynamic_slice_in_dim(dkey_sum, start, BLOCK, 0) + returned[0], start, 0
            )
            dvalue_sum = lax.dynamic_update_slice_in_dim(
                dvalue_sum,
                lax.dynamic_slice_in_dim(dvalue_sum, start, BLOCK, 0) + returned[1],
                start,
                0,
            )
        dkeys.append(dkey_sum.astype(jnp.bfloat16))
        dvalues.append(dvalue_sum.astype(jnp.bfloat16))
    dkey = jnp.concatenate(dkeys, axis=1)
    dvalue = jnp.concatenate(dvalues, axis=1)
    total = jnp.dot(dquery, w_query.T, preferred_element_type=jnp.float32)
    total = total + jnp.dot(dkey, w_key.T, preferred_element_type=jnp.float32)
    total = total + jnp.dot(dvalue, w_value.T, preferred_element_type=jnp.float32)
    grad_input = total.astype(jnp.bfloat16)
    sources = ((rows, dquery), (rows, dkey), (rows, dvalue), (attended, cot))
    grads = reduce_gradients(sources)
    return (result[None], grad_input[None]) + grads


def solution(mesh):
    return jax.shard_map(
        body,
        mesh=mesh,
        in_specs=(P("dp", "seq", None), P(), P(), P(), P(), P(), P("dp", "seq", None)),
        out_specs=(
            P("dp", "seq", None),
            P("dp", "seq", None),
            P("seq", None),
            P("seq", None),
            P("seq", None),
            P("seq", None),
        ),
        check_vma=False,
    )
```

```python
import functools

import jax
import jax.numpy as jnp
from jax import lax
from jax.experimental import pallas as pl
from jax.experimental.pallas import tpu as pltpu
from jax.sharding import PartitionSpec as P

HEADS = 16
BLOCK = 128
LANES = 128


def partner(array, axis, apart):
    return lax.ppermute(array, axis, [(i, i ^ 1 << apart) for i in range(lax.axis_size(axis))])


def swap_blocks(keys_local, values_local, offsets, levels, lo, hi):
    remote = []
    for level in range(levels):
        start = offsets[level] * BLOCK
        pair = jnp.stack(
            [
                lax.dynamic_slice_in_dim(keys_local[:, lo:hi], start, BLOCK, 0),
                lax.dynamic_slice_in_dim(values_local[:, lo:hi], start, BLOCK, 0),
            ]
        )
        remote.append(partner(pair, "seq", level))
    return remote


def attention_kernel(q_ref, k_ref, v_ref, do_ref, *refs, head, scale):
    remote = refs[:-5]
    att_ref, dq_ref, dk_ref, dv_ref, back_ref = refs[-5:]
    q = q_ref[...]
    k = jnp.concatenate([k_ref[...]] + [r[0] for r in remote], axis=0)
    v = jnp.concatenate([v_ref[...]] + [r[1] for r in remote], axis=0)
    do = do_ref[...]
    width = q.shape[1]
    lane = lax.broadcasted_iota(jnp.int32, (1, width), 1)
    row = lax.broadcasted_iota(jnp.int32, (width, 1), 0)
    q_t = q.T
    do_t = do.T
    probs, grads, v_parts, k_parts, q_parts, do_parts = [], [], [], [], [], []
    for j in range(width // head):
        inside = (lane >= j * head) & (lane < (j + 1) * head)
        rows_in = (row >= j * head) & (row < (j + 1) * head)
        qm = jnp.where(inside, q * jnp.asarray(scale, q.dtype), jnp.zeros_like(q))
        dom = jnp.where(inside, do, jnp.zeros_like(do))
        s = lax.dot_general(qm, k, (((1,), (1,)), ((), ())), preferred_element_type=jnp.float32)
        top = jnp.max(s, axis=-1, keepdims=True)
        e = jnp.exp(s - top)
        p = e * (1.0 / jnp.sum(e, axis=-1, keepdims=True))
        dp = lax.dot_general(dom, v, (((1,), (1,)), ((), ())), preferred_element_type=jnp.float32)
        delta = jnp.sum(p * dp, axis=-1, keepdims=True)
        probs.append(p.astype(jnp.bfloat16))
        grads.append((p * (dp - delta) * scale).astype(jnp.bfloat16))
        v_parts.append(jnp.where(inside, v, jnp.zeros_like(v)))
        k_parts.append(jnp.where(inside, k, jnp.zeros_like(k)))
        q_parts.append(jnp.where(rows_in, q_t, jnp.zeros_like(q_t)))
        do_parts.append(jnp.where(rows_in, do_t, jnp.zeros_like(do_t)))
    att = jnp.dot(jnp.concatenate(probs, 1), jnp.concatenate(v_parts, 0), preferred_element_type=jnp.float32)
    dq = jnp.dot(jnp.concatenate(grads, 1), jnp.concatenate(k_parts, 0), preferred_element_type=jnp.float32)
    dk_t = jnp.dot(jnp.concatenate(q_parts, 1), jnp.concatenate(grads, 0), preferred_element_type=jnp.float32)
    dv_t = jnp.dot(jnp.concatenate(do_parts, 1), jnp.concatenate(probs, 0), preferred_element_type=jnp.float32)
    att_ref[...] = att.astype(att_ref.dtype)
    dq_ref[...] = dq.astype(dq_ref.dtype)
    dk = dk_t.T
    dv = dv_t.T
    tok = q.shape[0]
    dk_ref[...] = dk[:tok]
    dv_ref[...] = dv[:tok]
    low = tok
    for level, r in enumerate(remote):
        high = low + r.shape[1]
        back_ref[level, 0] = dk[low:high].astype(back_ref.dtype)
        back_ref[level, 1] = dv[low:high].astype(back_ref.dtype)
        low = high


def attention(query, keys, values, d_att, remote, head, lo, hi):
    tok = query.shape[0]
    width = hi - lo
    levels = len(remote)
    block = remote[0].shape[1]
    total = tok + levels * block
    steps = width // LANES
    base = lo // LANES
    fspec = pl.BlockSpec((tok, LANES), lambda i: (0, i + base))
    qspec = pl.BlockSpec((tok, LANES), lambda i: (0, i))
    rspec = pl.BlockSpec((2, block, LANES), lambda i: (0, 0, i))
    bspec = pl.BlockSpec((levels, 2, block, LANES), lambda i: (0, 0, 0, i))
    return pl.pallas_call(
        functools.partial(attention_kernel, head=head, scale=head ** -0.5),
        grid=(steps,),
        in_specs=[fspec] * 4 + [rspec] * levels,
        out_specs=[qspec] * 4 + [bspec],
        out_shape=[
            jax.ShapeDtypeStruct((tok, width), jnp.bfloat16),
            jax.ShapeDtypeStruct((tok, width), jnp.bfloat16),
            jax.ShapeDtypeStruct((tok, width), jnp.float32),
            jax.ShapeDtypeStruct((tok, width), jnp.float32),
            jax.ShapeDtypeStruct((levels, 2, block, width), jnp.bfloat16),
        ],
        compiler_params=pltpu.CompilerParams(vmem_limit_bytes=60 * 1024 * 1024),
        cost_estimate=pl.CostEstimate(
            flops=12 * tok * total * width * (LANES // head),
            transcendentals=tok * total * (width // head),
            bytes_accessed=4 * tok * width + 12 * total * width,
        ),
    )(query, keys, values, d_att, *remote)


def exchange(array, axis, mask):
    return lax.ppermute(array, axis, [(i, i ^ mask) for i in range(lax.axis_size(axis))])


def add_bf16(a, b):
    return (a.astype(jnp.float32) + b.astype(jnp.float32)).astype(jnp.bfloat16)


def term(left, right, lo, hi):
    return jnp.dot(left.T, right[:, lo:hi], preferred_element_type=jnp.float32).astype(jnp.bfloat16)


def reduce_gradients(rows, dquery, attended, cot, late_fn, hold):
    n_dp = lax.axis_size("dp")
    n_seq = lax.axis_size("seq")
    seq_bits = n_seq.bit_length() - 1
    dp_bits = n_dp.bit_length() - 1
    width = dquery.shape[1]
    blk = rows.shape[1] // n_seq
    dp_i = lax.axis_index("dp")
    seq_i = lax.axis_index("seq")
    low = dp_i % 2 == 0

    def pick(a, b):
        return jnp.where(low, a, b)

    seq_dims = [("seq", b) for b in range(seq_bits)]
    dp_dims = [("dp", b) for b in range(1, dp_bits)]
    if seq_bits >= 2:
        orders = [
            seq_dims[:2] + dp_dims + seq_dims[2:],
            seq_dims[1::-1] + seq_dims[2:] + dp_dims,
        ]
    else:
        orders = [seq_dims + dp_dims] * 2
    shape = [2] * seq_bits + [2] * (dp_bits - 1) + [blk >> (dp_bits - 1)]

    def start(keep, send):
        got = exchange(term(*send, 0, width), "dp", 1)
        return add_bf16(term(*keep, 0, width), got).reshape(shape + [width])

    def steps(data, order, removed):
        for axis, b in order:
            if axis == "seq":
                at = seq_bits - 1 - b
                bit = (seq_i >> b) % 2
            else:
                at = seq_bits + (dp_bits - 1 - b)
                bit = (dp_i >> b) % 2
            at_now = at - sum(1 for r in removed if r < at)
            removed.append(at)
            kept = lax.dynamic_index_in_dim(data, bit, at_now, keepdims=False)
            out = lax.dynamic_index_in_dim(data, 1 - bit, at_now, keepdims=False)
            data = add_bf16(kept, exchange(out, axis, 1 << b))
        return data

    early = start((pick(rows, attended), pick(dquery, cot)), (pick(attended, rows), pick(cot, dquery)))
    removed_early = []
    early = steps(early, orders[0][:1], removed_early)
    early, hold = lax.optimization_barrier((early, hold))
    dkey, dvalue = late_fn(hold)
    late = start((rows, pick(dkey, dvalue)), (rows, pick(dvalue, dkey)))
    late = steps(late, orders[1], [])
    early = steps(early, orders[0][1:], removed_early)
    data = jnp.concatenate([early, late], axis=1)
    for b in range(1, dp_bits):
        recv = exchange(data, "dp", 1 << b)
        first_half = (dp_i >> b) % 2 == 0
        data = jnp.where(first_half, jnp.concatenate([data, recv], 0), jnp.concatenate([recv, data], 0))
    back = exchange(data, "dp", 1)
    mine = [data[:, :width], data[:, width:]]
    other = [back[:, :width], back[:, width:]]
    query = pick(mine[0], other[0])
    outw = pick(other[0], mine[0])
    key = pick(mine[1], other[1])
    value = pick(other[1], mine[1])
    grads = tuple(g.astype(jnp.float32) for g in (query, key, value, outw))
    return grads, dkey, dvalue


def body(layer_input, w_query, w_key, w_value, w_out, offsets, grad_out):
    rows = layer_input[0]
    cot = grad_out[0]
    tok = rows.shape[0]
    width = rows.shape[1]
    head = width // HEADS
    levels = lax.axis_size("seq").bit_length() - 1
    query = jnp.dot(rows, w_query, preferred_element_type=jnp.float32).astype(jnp.bfloat16)
    keys_local = jnp.dot(rows, w_key, preferred_element_type=jnp.float32).astype(jnp.bfloat16)
    values_local = jnp.dot(rows, w_value, preferred_element_type=jnp.float32).astype(jnp.bfloat16)
    half = (width // LANES) // 2 * LANES
    spans = [(0, half), (half, width)]
    remotes = [swap_blocks(keys_local, values_local, offsets, levels, *spans[0])]
    later_keys, later_values, _ = lax.optimization_barrier((keys_local, values_local, remotes[0]))
    remotes.append(swap_blocks(later_keys, later_values, offsets, levels, *spans[1]))
    d_att = jnp.dot(cot, w_out.T, preferred_element_type=jnp.float32).astype(jnp.bfloat16)
    outs = [
        attention(query, keys_local, values_local, d_att, remote, head, lo, hi)
        for remote, (lo, hi) in zip(remotes, spans)
    ]
    attended = jnp.concatenate([o[0] for o in outs], axis=1)
    dquery = jnp.concatenate([o[1] for o in outs], axis=1)
    result = jnp.dot(attended, w_out, preferred_element_type=jnp.float32).astype(jnp.bfloat16)
    returned_all = [
        [partner(back[level], "seq", level) for level in range(levels)] for _, _, _, _, back in outs
    ]

    def late_fn(returned_all):
        dkeys = []
        dvalues = []
        for (_, _, dkey_sum, dvalue_sum, _), returned_list in zip(outs, returned_all):
            for level in range(levels):
                returned = returned_list[level].astype(jnp.float32)
                start = offsets[level] * BLOCK
                dkey_sum = lax.dynamic_update_slice_in_dim(
                    dkey_sum, lax.dynamic_slice_in_dim(dkey_sum, start, BLOCK, 0) + returned[0], start, 0
                )
                dvalue_sum = lax.dynamic_update_slice_in_dim(
                    dvalue_sum,
                    lax.dynamic_slice_in_dim(dvalue_sum, start, BLOCK, 0) + returned[1],
                    start,
                    0,
                )
            dkeys.append(dkey_sum.astype(jnp.bfloat16))
            dvalues.append(dvalue_sum.astype(jnp.bfloat16))
        return jnp.concatenate(dkeys, axis=1), jnp.concatenate(dvalues, axis=1)

    grads, dkey, dvalue = reduce_gradients(rows, dquery, attended, cot, late_fn, returned_all)
    total = jnp.dot(dquery, w_query.T, preferred_element_type=jnp.float32)
    total = total + jnp.dot(dkey, w_key.T, preferred_element_type=jnp.float32)
    total = total + jnp.dot(dvalue, w_value.T, preferred_element_type=jnp.float32)
    grad_input = total.astype(jnp.bfloat16)
    return (result[None], grad_input[None]) + grads


def solution(mesh):
    return jax.shard_map(
        body,
        mesh=mesh,
        in_specs=(P("dp", "seq", None), P(), P(), P(), P(), P(), P("dp", "seq", None)),
        out_specs=(
            P("dp", "seq", None),
            P("dp", "seq", None),
            P("seq", None),
            P("seq", None),
            P("seq", None),
            P("seq", None),
        ),
        check_vma=False,
    )
```

```python
import functools

import jax
import jax.numpy as jnp
from jax import lax
from jax.experimental import pallas as pl
from jax.experimental.pallas import tpu as pltpu
from jax.sharding import PartitionSpec as P

HEADS = 16
BLOCK = 128
LANES = 128


def partner(array, axis, apart):
    return lax.ppermute(array, axis, [(i, i ^ 1 << apart) for i in range(lax.axis_size(axis))])


def swap_blocks(keys_local, values_local, offsets, levels, lo, hi):
    remote = []
    for level in range(levels):
        start = offsets[level] * BLOCK
        pair = jnp.stack(
            [
                lax.dynamic_slice_in_dim(keys_local[:, lo:hi], start, BLOCK, 0),
                lax.dynamic_slice_in_dim(values_local[:, lo:hi], start, BLOCK, 0),
            ]
        )
        remote.append(partner(pair, "seq", level))
    return remote


def attention_kernel(q_ref, k_ref, v_ref, do_ref, *refs, head, scale):
    remote = refs[:-5]
    att_ref, dq_ref, dk_ref, dv_ref, back_ref = refs[-5:]
    q = q_ref[...]
    k = jnp.concatenate([k_ref[...]] + [r[0] for r in remote], axis=0)
    v = jnp.concatenate([v_ref[...]] + [r[1] for r in remote], axis=0)
    do = do_ref[...]
    width = q.shape[1]
    lane = lax.broadcasted_iota(jnp.int32, (1, width), 1)
    row = lax.broadcasted_iota(jnp.int32, (width, 1), 0)
    q_t = q.T
    do_t = do.T
    probs, grads, v_parts, k_parts, q_parts, do_parts = [], [], [], [], [], []
    for j in range(width // head):
        inside = (lane >= j * head) & (lane < (j + 1) * head)
        rows_in = (row >= j * head) & (row < (j + 1) * head)
        qm = jnp.where(inside, q * jnp.asarray(scale, q.dtype), jnp.zeros_like(q))
        dom = jnp.where(inside, do, jnp.zeros_like(do))
        s = lax.dot_general(qm, k, (((1,), (1,)), ((), ())), preferred_element_type=jnp.float32)
        top = jnp.max(s, axis=-1, keepdims=True)
        e = jnp.exp(s - top)
        p = e * (1.0 / jnp.sum(e, axis=-1, keepdims=True))
        dp = lax.dot_general(dom, v, (((1,), (1,)), ((), ())), preferred_element_type=jnp.float32)
        delta = jnp.sum(p * dp, axis=-1, keepdims=True)
        probs.append(p.astype(jnp.bfloat16))
        grads.append((p * (dp - delta) * scale).astype(jnp.bfloat16))
        v_parts.append(jnp.where(inside, v, jnp.zeros_like(v)))
        k_parts.append(jnp.where(inside, k, jnp.zeros_like(k)))
        q_parts.append(jnp.where(rows_in, q_t, jnp.zeros_like(q_t)))
        do_parts.append(jnp.where(rows_in, do_t, jnp.zeros_like(do_t)))
    att = jnp.dot(jnp.concatenate(probs, 1), jnp.concatenate(v_parts, 0), preferred_element_type=jnp.float32)
    dq = jnp.dot(jnp.concatenate(grads, 1), jnp.concatenate(k_parts, 0), preferred_element_type=jnp.float32)
    dk_t = jnp.dot(jnp.concatenate(q_parts, 1), jnp.concatenate(grads, 0), preferred_element_type=jnp.float32)
    dv_t = jnp.dot(jnp.concatenate(do_parts, 1), jnp.concatenate(probs, 0), preferred_element_type=jnp.float32)
    att_ref[...] = att.astype(att_ref.dtype)
    dq_ref[...] = dq.astype(dq_ref.dtype)
    dk = dk_t.T
    dv = dv_t.T
    tok = q.shape[0]
    dk_ref[...] = dk[:tok]
    dv_ref[...] = dv[:tok]
    low = tok
    for level, r in enumerate(remote):
        high = low + r.shape[1]
        back_ref[level, 0] = dk[low:high].astype(back_ref.dtype)
        back_ref[level, 1] = dv[low:high].astype(back_ref.dtype)
        low = high


def attention(query, keys, values, d_att, remote, head, lo, hi):
    tok = query.shape[0]
    width = hi - lo
    levels = len(remote)
    block = remote[0].shape[1]
    total = tok + levels * block
    steps = width // LANES
    base = lo // LANES
    fspec = pl.BlockSpec((tok, LANES), lambda i: (0, i + base))
    qspec = pl.BlockSpec((tok, LANES), lambda i: (0, i))
    rspec = pl.BlockSpec((2, block, LANES), lambda i: (0, 0, i))
    bspec = pl.BlockSpec((levels, 2, block, LANES), lambda i: (0, 0, 0, i))
    return pl.pallas_call(
        functools.partial(attention_kernel, head=head, scale=head ** -0.5),
        grid=(steps,),
        in_specs=[fspec] * 4 + [rspec] * levels,
        out_specs=[qspec] * 4 + [bspec],
        out_shape=[
            jax.ShapeDtypeStruct((tok, width), jnp.bfloat16),
            jax.ShapeDtypeStruct((tok, width), jnp.bfloat16),
            jax.ShapeDtypeStruct((tok, width), jnp.float32),
            jax.ShapeDtypeStruct((tok, width), jnp.float32),
            jax.ShapeDtypeStruct((levels, 2, block, width), jnp.bfloat16),
        ],
        compiler_params=pltpu.CompilerParams(vmem_limit_bytes=60 * 1024 * 1024),
        cost_estimate=pl.CostEstimate(
            flops=12 * tok * total * width * (LANES // head),
            transcendentals=tok * total * (width // head),
            bytes_accessed=4 * tok * width + 12 * total * width,
        ),
    )(query, keys, values, d_att, *remote)


def exchange(array, axis, mask):
    return lax.ppermute(array, axis, [(i, i ^ mask) for i in range(lax.axis_size(axis))])


def add_bf16(a, b):
    return (a.astype(jnp.float32) + b.astype(jnp.float32)).astype(jnp.bfloat16)


def term(left, right, lo, hi):
    return jnp.dot(left.T, right[:, lo:hi], preferred_element_type=jnp.float32).astype(jnp.bfloat16)


def reduce_gradients(sources):
    n_dp = lax.axis_size("dp")
    n_seq = lax.axis_size("seq")
    seq_bits = n_seq.bit_length() - 1
    dp_bits = n_dp.bit_length() - 1
    width = sources[0][1].shape[1]
    rows = sources[0][0].shape[1]
    blk = rows // n_seq
    dp_i = lax.axis_index("dp")
    seq_i = lax.axis_index("seq")
    low = dp_i % 2 == 0

    def pick(a, b):
        return jnp.where(low, a, b)

    keep = [
        (sources[0][0], pick(sources[0][1], sources[2][1])),
        (pick(sources[1][0], sources[3][0]), pick(sources[1][1], sources[3][1])),
    ]
    send = [
        (sources[2][0], pick(sources[2][1], sources[0][1])),
        (pick(sources[3][0], sources[1][0]), pick(sources[3][1], sources[1][1])),
    ]
    seq_dims = [("seq", b) for b in range(seq_bits)]
    dp_dims = [("dp", b) for b in range(1, dp_bits)]
    if seq_bits >= 2:
        orders = [
            seq_dims[:2] + dp_dims + seq_dims[2:],
            dp_dims + seq_dims,
        ]
    else:
        orders = [seq_dims + dp_dims] * 2
    shape = [2] * seq_bits + [2] * (dp_bits - 1) + [blk >> (dp_bits - 1)]
    sends = [term(*send[g], 0, width) for g in range(2)]
    keeps = [term(*keep[g], 0, width) for g in range(2)]
    got = exchange(sends, "dp", 1)
    pieces = []
    for g in range(2):
        data = add_bf16(keeps[g], got[g]).reshape(shape + [width])
        removed = []
        for axis, b in orders[g]:
            if axis == "seq":
                at = seq_bits - 1 - b
                bit = (seq_i >> b) % 2
            else:
                at = seq_bits + (dp_bits - 1 - b)
                bit = (dp_i >> b) % 2
            at_now = at - sum(1 for r in removed if r < at)
            removed.append(at)
            kept = lax.dynamic_index_in_dim(data, bit, at_now, keepdims=False)
            out = lax.dynamic_index_in_dim(data, 1 - bit, at_now, keepdims=False)
            data = add_bf16(kept, exchange(out, axis, 1 << b))
        pieces.append(data)
    data = jnp.concatenate(pieces, axis=1)
    for b in range(1, dp_bits):
        recv = exchange(data, "dp", 1 << b)
        first_half = (dp_i >> b) % 2 == 0
        data = jnp.where(first_half, jnp.concatenate([data, recv], 0), jnp.concatenate([recv, data], 0))
    pieces = [data]
    part = jnp.concatenate(pieces, axis=1)
    back = exchange(part, "dp", 1)
    mine = [part[:, :width], part[:, width:]]
    other = [back[:, :width], back[:, width:]]
    return (
        pick(mine[0], other[0]).astype(jnp.float32),
        pick(mine[1], other[1]).astype(jnp.float32),
        pick(other[0], mine[0]).astype(jnp.float32),
        pick(other[1], mine[1]).astype(jnp.float32),
    )


def body(layer_input, w_query, w_key, w_value, w_out, offsets, grad_out):
    rows = layer_input[0]
    cot = grad_out[0]
    tok = rows.shape[0]
    width = rows.shape[1]
    head = width // HEADS
    levels = lax.axis_size("seq").bit_length() - 1
    query = jnp.dot(rows, w_query, preferred_element_type=jnp.float32).astype(jnp.bfloat16)
    keys_local = jnp.dot(rows, w_key, preferred_element_type=jnp.float32).astype(jnp.bfloat16)
    values_local = jnp.dot(rows, w_value, preferred_element_type=jnp.float32).astype(jnp.bfloat16)
    half = (width // LANES) // 2 * LANES
    spans = [(0, half), (half, width)]
    remotes = [swap_blocks(keys_local, values_local, offsets, levels, *spans[0])]
    later_keys, later_values, _ = lax.optimization_barrier((keys_local, values_local, remotes[0]))
    remotes.append(swap_blocks(later_keys, later_values, offsets, levels, *spans[1]))
    d_att = jnp.dot(cot, w_out.T, preferred_element_type=jnp.float32).astype(jnp.bfloat16)
    outs = [
        attention(query, keys_local, values_local, d_att, remote, head, lo, hi)
        for remote, (lo, hi) in zip(remotes, spans)
    ]
    attended = jnp.concatenate([o[0] for o in outs], axis=1)
    dquery = jnp.concatenate([o[1] for o in outs], axis=1)
    result = jnp.dot(attended, w_out, preferred_element_type=jnp.float32).astype(jnp.bfloat16)
    dkeys = []
    dvalues = []
    for _, _, dkey_sum, dvalue_sum, back in outs:
        for level in range(levels):
            returned = partner(back[level], "seq", level).astype(jnp.float32)
            start = offsets[level] * BLOCK
            dkey_sum = lax.dynamic_update_slice_in_dim(
                dkey_sum, lax.dynamic_slice_in_dim(dkey_sum, start, BLOCK, 0) + returned[0], start, 0
            )
            dvalue_sum = lax.dynamic_update_slice_in_dim(
                dvalue_sum,
                lax.dynamic_slice_in_dim(dvalue_sum, start, BLOCK, 0) + returned[1],
                start,
                0,
            )
        dkeys.append(dkey_sum.astype(jnp.bfloat16))
        dvalues.append(dvalue_sum.astype(jnp.bfloat16))
    dkey = jnp.concatenate(dkeys, axis=1)
    dvalue = jnp.concatenate(dvalues, axis=1)
    total = jnp.dot(dquery, w_query.T, preferred_element_type=jnp.float32)
    total = total + jnp.dot(dkey, w_key.T, preferred_element_type=jnp.float32)
    total = total + jnp.dot(dvalue, w_value.T, preferred_element_type=jnp.float32)
    grad_input = total.astype(jnp.bfloat16)
    sources = ((rows, dquery), (rows, dkey), (rows, dvalue), (attended, cot))
    grads = reduce_gradients(sources)
    return (result[None], grad_input[None]) + grads


def solution(mesh):
    return jax.shard_map(
        body,
        mesh=mesh,
        in_specs=(P("dp", "seq", None), P(), P(), P(), P(), P(), P("dp", "seq", None)),
        out_specs=(
            P("dp", "seq", None),
            P("dp", "seq", None),
            P("seq", None),
            P("seq", None),
            P("seq", None),
            P("seq", None),
        ),
        check_vma=False,
    )
```

```python
import functools

import jax
import jax.numpy as jnp
from jax import lax
from jax.experimental import pallas as pl
from jax.experimental.pallas import tpu as pltpu
from jax.sharding import PartitionSpec as P

HEADS = 16
BLOCK = 128
LANES = 128


def partner(array, axis, apart):
    return lax.ppermute(array, axis, [(i, i ^ 1 << apart) for i in range(lax.axis_size(axis))])


def swap_blocks(keys_local, values_local, offsets, levels, lo, hi):
    remote = []
    for level in range(levels):
        start = offsets[level] * BLOCK
        pair = jnp.stack(
            [
                lax.dynamic_slice_in_dim(keys_local[:, lo:hi], start, BLOCK, 0),
                lax.dynamic_slice_in_dim(values_local[:, lo:hi], start, BLOCK, 0),
            ]
        )
        remote.append(partner(pair, "seq", level))
    return remote


def attention_kernel(q_ref, k_ref, v_ref, do_ref, *refs, head, scale):
    remote = refs[:-5]
    att_ref, dq_ref, dk_ref, dv_ref, back_ref = refs[-5:]
    q = q_ref[...]
    k = jnp.concatenate([k_ref[...]] + [r[0] for r in remote], axis=0)
    v = jnp.concatenate([v_ref[...]] + [r[1] for r in remote], axis=0)
    do = do_ref[...]
    width = q.shape[1]
    lane = lax.broadcasted_iota(jnp.int32, (1, width), 1)
    row = lax.broadcasted_iota(jnp.int32, (width, 1), 0)
    q_t = q.T
    do_t = do.T
    probs, grads, v_parts, k_parts, q_parts, do_parts = [], [], [], [], [], []
    for j in range(width // head):
        inside = (lane >= j * head) & (lane < (j + 1) * head)
        rows_in = (row >= j * head) & (row < (j + 1) * head)
        qm = jnp.where(inside, q * jnp.asarray(scale, q.dtype), jnp.zeros_like(q))
        dom = jnp.where(inside, do, jnp.zeros_like(do))
        s = lax.dot_general(qm, k, (((1,), (1,)), ((), ())), preferred_element_type=jnp.float32)
        top = jnp.max(s, axis=-1, keepdims=True)
        e = jnp.exp(s - top)
        p = e * (1.0 / jnp.sum(e, axis=-1, keepdims=True))
        dp = lax.dot_general(dom, v, (((1,), (1,)), ((), ())), preferred_element_type=jnp.float32)
        delta = jnp.sum(p * dp, axis=-1, keepdims=True)
        probs.append(p.astype(jnp.bfloat16))
        grads.append((p * (dp - delta) * scale).astype(jnp.bfloat16))
        v_parts.append(jnp.where(inside, v, jnp.zeros_like(v)))
        k_parts.append(jnp.where(inside, k, jnp.zeros_like(k)))
        q_parts.append(jnp.where(rows_in, q_t, jnp.zeros_like(q_t)))
        do_parts.append(jnp.where(rows_in, do_t, jnp.zeros_like(do_t)))
    att = jnp.dot(jnp.concatenate(probs, 1), jnp.concatenate(v_parts, 0), preferred_element_type=jnp.float32)
    dq = jnp.dot(jnp.concatenate(grads, 1), jnp.concatenate(k_parts, 0), preferred_element_type=jnp.float32)
    dk_t = jnp.dot(jnp.concatenate(q_parts, 1), jnp.concatenate(grads, 0), preferred_element_type=jnp.float32)
    dv_t = jnp.dot(jnp.concatenate(do_parts, 1), jnp.concatenate(probs, 0), preferred_element_type=jnp.float32)
    att_ref[...] = att.astype(att_ref.dtype)
    dq_ref[...] = dq.astype(dq_ref.dtype)
    dk = dk_t.T
    dv = dv_t.T
    tok = q.shape[0]
    dk_ref[...] = dk[:tok]
    dv_ref[...] = dv[:tok]
    low = tok
    for level, r in enumerate(remote):
        high = low + r.shape[1]
        back_ref[level, 0] = dk[low:high].astype(back_ref.dtype)
        back_ref[level, 1] = dv[low:high].astype(back_ref.dtype)
        low = high


def attention(query, keys, values, d_att, remote, head, lo, hi):
    tok = query.shape[0]
    width = hi - lo
    levels = len(remote)
    block = remote[0].shape[1]
    total = tok + levels * block
    steps = width // LANES
    base = lo // LANES
    fspec = pl.BlockSpec((tok, LANES), lambda i: (0, i + base))
    qspec = pl.BlockSpec((tok, LANES), lambda i: (0, i))
    rspec = pl.BlockSpec((2, block, LANES), lambda i: (0, 0, i))
    bspec = pl.BlockSpec((levels, 2, block, LANES), lambda i: (0, 0, 0, i))
    return pl.pallas_call(
        functools.partial(attention_kernel, head=head, scale=head ** -0.5),
        grid=(steps,),
        in_specs=[fspec] * 4 + [rspec] * levels,
        out_specs=[qspec] * 4 + [bspec],
        out_shape=[
            jax.ShapeDtypeStruct((tok, width), jnp.bfloat16),
            jax.ShapeDtypeStruct((tok, width), jnp.bfloat16),
            jax.ShapeDtypeStruct((tok, width), jnp.float32),
            jax.ShapeDtypeStruct((tok, width), jnp.float32),
            jax.ShapeDtypeStruct((levels, 2, block, width), jnp.bfloat16),
        ],
        compiler_params=pltpu.CompilerParams(vmem_limit_bytes=60 * 1024 * 1024),
        cost_estimate=pl.CostEstimate(
            flops=12 * tok * total * width * (LANES // head),
            transcendentals=tok * total * (width // head),
            bytes_accessed=4 * tok * width + 12 * total * width,
        ),
    )(query, keys, values, d_att, *remote)


def exchange(array, axis, mask):
    return lax.ppermute(array, axis, [(i, i ^ mask) for i in range(lax.axis_size(axis))])


def add_bf16(a, b):
    return (a.astype(jnp.float32) + b.astype(jnp.float32)).astype(jnp.bfloat16)


def term(left, right, lo, hi):
    return jnp.dot(left.T, right[:, lo:hi], preferred_element_type=jnp.float32).astype(jnp.bfloat16)


def reduce_gradients(sources):
    n_dp = lax.axis_size("dp")
    n_seq = lax.axis_size("seq")
    seq_bits = n_seq.bit_length() - 1
    dp_bits = n_dp.bit_length() - 1
    width = sources[0][1].shape[1]
    rows = sources[0][0].shape[1]
    blk = rows // n_seq
    dp_i = lax.axis_index("dp")
    seq_i = lax.axis_index("seq")
    low = dp_i % 2 == 0

    def pick(a, b):
        return jnp.where(low, a, b)

    keep = [
        (sources[0][0], pick(sources[0][1], sources[2][1])),
        (pick(sources[1][0], sources[3][0]), pick(sources[1][1], sources[3][1])),
    ]
    send = [
        (sources[2][0], pick(sources[2][1], sources[0][1])),
        (pick(sources[3][0], sources[1][0]), pick(sources[3][1], sources[1][1])),
    ]
    seq_dims = [("seq", b) for b in range(seq_bits)]
    dp_dims = [("dp", b) for b in range(1, dp_bits)]
    if seq_bits >= 2:
        orders = [
            seq_dims[:2] + dp_dims + seq_dims[2:],
            dp_dims + seq_dims,
        ]
    else:
        orders = [seq_dims + dp_dims] * 2
    shape = [2] * seq_bits + [2] * (dp_bits - 1) + [blk >> (dp_bits - 1)]
    sends = [term(*send[g], 0, width) for g in range(2)]
    keeps = [term(*keep[g], 0, width) for g in range(2)]
    got = exchange(sends, "dp", 1)
    pieces = []
    for g in range(2):
        data = add_bf16(keeps[g], got[g]).reshape(shape + [width])
        removed = []
        for axis, b in orders[g]:
            if axis == "seq":
                at = seq_bits - 1 - b
                bit = (seq_i >> b) % 2
            else:
                at = seq_bits + (dp_bits - 1 - b)
                bit = (dp_i >> b) % 2
            at_now = at - sum(1 for r in removed if r < at)
            removed.append(at)
            kept = lax.dynamic_index_in_dim(data, bit, at_now, keepdims=False)
            out = lax.dynamic_index_in_dim(data, 1 - bit, at_now, keepdims=False)
            data = add_bf16(kept, exchange(out, axis, 1 << b))
        pieces.append(data)
    data = jnp.concatenate(pieces, axis=1)
    for b in range(1, dp_bits):
        recv = exchange(data, "dp", 1 << b)
        first_half = (dp_i >> b) % 2 == 0
        data = jnp.where(first_half, jnp.concatenate([data, recv], 0), jnp.concatenate([recv, data], 0))
    pieces = [data]
    part = jnp.concatenate(pieces, axis=1)
    back = exchange(part, "dp", 1)
    mine = [part[:, :width], part[:, width:]]
    other = [back[:, :width], back[:, width:]]
    return (
        pick(mine[0], other[0]).astype(jnp.float32),
        pick(mine[1], other[1]).astype(jnp.float32),
        pick(other[0], mine[0]).astype(jnp.float32),
        pick(other[1], mine[1]).astype(jnp.float32),
    )


def body(layer_input, w_query, w_key, w_value, w_out, offsets, grad_out):
    rows = layer_input[0]
    cot = grad_out[0]
    tok = rows.shape[0]
    width = rows.shape[1]
    head = width // HEADS
    levels = lax.axis_size("seq").bit_length() - 1
    query = jnp.dot(rows, w_query, preferred_element_type=jnp.float32).astype(jnp.bfloat16)
    keys_local = jnp.dot(rows, w_key, preferred_element_type=jnp.float32).astype(jnp.bfloat16)
    values_local = jnp.dot(rows, w_value, preferred_element_type=jnp.float32).astype(jnp.bfloat16)
    half = (width // LANES) * 3 // 8 * LANES
    spans = [(0, half), (half, width)]
    remotes = [swap_blocks(keys_local, values_local, offsets, levels, *spans[0])]
    later_keys, later_values, _ = lax.optimization_barrier((keys_local, values_local, remotes[0]))
    remotes.append(swap_blocks(later_keys, later_values, offsets, levels, *spans[1]))
    d_att = jnp.dot(cot, w_out.T, preferred_element_type=jnp.float32).astype(jnp.bfloat16)
    outs = [
        attention(query, keys_local, values_local, d_att, remote, head, lo, hi)
        for remote, (lo, hi) in zip(remotes, spans)
    ]
    attended = jnp.concatenate([o[0] for o in outs], axis=1)
    dquery = jnp.concatenate([o[1] for o in outs], axis=1)
    result = jnp.dot(attended, w_out, preferred_element_type=jnp.float32).astype(jnp.bfloat16)
    dkeys = []
    dvalues = []
    for _, _, dkey_sum, dvalue_sum, back in outs:
        for level in range(levels):
            returned = partner(back[level], "seq", level).astype(jnp.float32)
            start = offsets[level] * BLOCK
            dkey_sum = lax.dynamic_update_slice_in_dim(
                dkey_sum, lax.dynamic_slice_in_dim(dkey_sum, start, BLOCK, 0) + returned[0], start, 0
            )
            dvalue_sum = lax.dynamic_update_slice_in_dim(
                dvalue_sum,
                lax.dynamic_slice_in_dim(dvalue_sum, start, BLOCK, 0) + returned[1],
                start,
                0,
            )
        dkeys.append(dkey_sum.astype(jnp.bfloat16))
        dvalues.append(dvalue_sum.astype(jnp.bfloat16))
    dkey = jnp.concatenate(dkeys, axis=1)
    dvalue = jnp.concatenate(dvalues, axis=1)
    total = jnp.dot(dquery, w_query.T, preferred_element_type=jnp.float32)
    total = total + jnp.dot(dkey, w_key.T, preferred_element_type=jnp.float32)
    total = total + jnp.dot(dvalue, w_value.T, preferred_element_type=jnp.float32)
    grad_input = total.astype(jnp.bfloat16)
    sources = ((rows, dquery), (rows, dkey), (rows, dvalue), (attended, cot))
    grads = reduce_gradients(sources)
    return (result[None], grad_input[None]) + grads


def solution(mesh):
    return jax.shard_map(
        body,
        mesh=mesh,
        in_specs=(P("dp", "seq", None), P(), P(), P(), P(), P(), P("dp", "seq", None)),
        out_specs=(
            P("dp", "seq", None),
            P("dp", "seq", None),
            P("seq", None),
            P("seq", None),
            P("seq", None),
            P("seq", None),
        ),
        check_vma=False,
    )
```
